128 devices in a mesh: leaf: 16 (over y, z), ctx: 8 (over x, core).
Axes of the slice: x: 4, y: 4, z: 4, core: 2. Of those that a mesh axis runs over, the one named last changes fastest.
Arguments:
- query_key_value_rows: bfloat16 [16384, 7168], P(('leaf', 'ctx')), may hold values from -6 to 6
- cotangent: bfloat16 [16384, 5120], P(('leaf', 'ctx')), may hold values from -6 to 6
- out_weight: bfloat16 [5120, 5120], P('ctx'), may hold values from -0.078125 to 0.078125
- parents: int32 [16, 8], P('leaf'), may hold values from 0 to 6, as said below
- rollout_spans: int32 [16384], P('leaf'), may hold values from 64 to 4096
Outputs:
- qkv_grad: bfloat16 [16384, 7168], P(('leaf', 'ctx'))
- weight_grad: bfloat16 [5120, 5120], P('ctx')
The draws below stay inside these ranges and needn't reach their ends.
Inputs may be any that keep to these rules, and one draw needn't show every extreme that they name: parents[t, 0] = 0, every later block's parent is an earlier block of the same tree, and the last block's parent is the block just before it.
All inputs are finite; a program needn't handle non-finite values.
Results may differ from the reference program's by a relative error of at most 0.012.
The reference program's roundings to bfloat16 on the way count: a program that leaves them out, or rounds other values in their place, can miss the bound.
Values may be sent and summed in bfloat16 or wider, within the bound.
No kernel may reach another device: no remote copies, remote signals or barrier semaphores. Data moves between devices by JAX's collectives and lax.ppermute only.
A program may use at most 192 MiB of HBM per device.

```python
import math
import jax
import jax.numpy as jnp
from jax import lax

D = 5120
QUERY_HEADS = 40
KEY_VALUE_HEADS = 8
HEAD_SIZE = 128
BLK = 128
TREE_TOKENS = 1024
NBLK = 8
PACKED_TREES = 16
ROWS = 16384
QKV_W = 7168


def draw_parents(key, part):
    raw_draw = jax.random.randint(key, (PACKED_TREES, NBLK), 0, 1 << 20)
    limits = jnp.maximum(jnp.arange(NBLK, dtype=jnp.int32), 1)
    drawn = (raw_draw % limits[None, :]).astype(jnp.int32)
    block_index = jnp.arange(NBLK, dtype=jnp.int32)
    return jnp.where(block_index[None, :] == NBLK - 1, NBLK - 2, drawn).astype(jnp.int32)


def draw_query_key_value_rows(key, part):
    values = jnp.clip(jax.random.normal(key, (ROWS, QKV_W), jnp.float32), -4.0, 4.0)
    return values.astype(jnp.bfloat16)


def plant(array, own_key, low, largest):
    place = [jax.random.randint(jax.random.fold_in(own_key, axis), (), 0, length) for axis, length in enumerate(array.shape)]
    longest = array.shape.index(max(array.shape))
    neighbour = place[:longest] + [(place[longest] + 1) % array.shape[longest]] + place[longest + 1:]
    return array.at[tuple(place)].set(low).at[tuple(neighbour)].set(largest)


def levels(own_key, shape, shards, least, top_value):
    level = 1.0
    for dim, parts in shards:
        draws = jax.random.uniform(jax.random.fold_in(jax.random.fold_in(own_key, 6), dim), (parts,), jnp.float32, least / len(shards), top_value / len(shards))
        level = level * jnp.repeat(jnp.exp(draws), shape[dim] // parts).reshape((-1,) + (1,) * (len(shape) - 1 - dim))
    return level


def noise(stream_key, shape, width, most, shards=(), kind=jnp.bfloat16):
    entries = jax.random.normal(stream_key, shape, jnp.float32) * width
    if len(shards) > 0:
        entries = levels(stream_key, shape, shards, -0.22, 0.18) * entries
    return jnp.clip(entries, min=-most, max=most).astype(kind)


def setup_inputs(seed: int = 0) -> dict:
    seeds = jax.random.split(jax.random.key(seed), 6)
    query_key_value_rows = draw_query_key_value_rows(jax.random.fold_in(seeds[5], 71), 0)
    cotangent = noise(seeds[1], (ROWS, D), 1.0, 6.0, ((0, 128),))
    out_weight = noise(seeds[2], (QUERY_HEADS * HEAD_SIZE, D), (QUERY_HEADS * HEAD_SIZE) ** -0.5, 0.078125, ((0, 8),))
    parents = draw_parents(jax.random.fold_in(seeds[5], 71), 0)
    rollout_spans = plant(jax.random.randint(seeds[4], (ROWS,), 64, 4097), jax.random.fold_in(seeds[4], 1), 64, 4096).astype(jnp.int32)
    return {"query_key_value_rows": query_key_value_rows, "cotangent": cotangent, "out_weight": out_weight, "parents": parents, "rollout_spans": rollout_spans}


log_base = 1024.0

def ancestors(parents):
    number = parents.shape[0]
    indices = jnp.arange(number, dtype=jnp.int32)

    def advance(iteration, state):
        current, reached = state
        current = lax.optimization_barrier(jnp.sum(jnp.where(current[:, None] == indices[None, :], parents[None, :], 0), axis=1)).astype(jnp.int32)
        return (current, reached | (current[:, None] == indices[None, :]))
    return lax.fori_loop(0, number, advance, (indices, indices[:, None] == indices[None, :]))[1]

def token_mask(reached, first_row, query_count, key_count):
    query_pos = first_row + jnp.arange(query_count, dtype=jnp.int32)
    key_pos = jnp.arange(key_count, dtype=jnp.int32)
    block_part = reached[first_row // BLK:(first_row + query_count) // BLK, :key_count // BLK]
    expanded = jnp.repeat(jnp.repeat(block_part, BLK, axis=0), BLK, axis=1)
    same_block = (query_pos // BLK)[:, None] == (key_pos // BLK)[None, :]
    return expanded & (jnp.logical_not(same_block) | (key_pos[None, :] <= query_pos[:, None]))

def span_softness(rollout_spans):
    return jnp.log(rollout_spans.astype(jnp.float32)) * (1.0 / (math.log(log_base) * math.sqrt(HEAD_SIZE)))

def reference(query_key_value_rows, cotangent, out_weight, parents, rollout_spans):
    queries_per_group = QUERY_HEADS // KEY_VALUE_HEADS
    every_row = query_key_value_rows.reshape(PACKED_TREES, TREE_TOKENS, KEY_VALUE_HEADS, queries_per_group + 2, HEAD_SIZE)
    cot_all = cotangent.reshape(PACKED_TREES, TREE_TOKENS, D)
    len_all = rollout_spans.reshape(PACKED_TREES, TREE_TOKENS)

    def one_tree(inputs):
        grouped, upstream, parent_ids, rollout_span_lookup = inputs
        allowed = token_mask(ancestors(parent_ids), 0, TREE_TOKENS, TREE_TOKENS)
        softness_multiplier = span_softness(rollout_span_lookup)
        asking_matrix = grouped[:, :, :queries_per_group].astype(jnp.float32)
        lookup_matrix = grouped[:, :, queries_per_group].astype(jnp.float32)
        values = grouped[:, :, queries_per_group + 1].astype(jnp.float32)
        attention_logits = jnp.einsum('zpyr,kpr->pyzk', asking_matrix, lookup_matrix) * softness_multiplier[None, None, :, None]
        attention_logits = jnp.where(allowed[None, None], attention_logits, -jnp.inf)
        peak_score = lax.optimization_barrier(jnp.max(attention_logits, axis=-1, keepdims=True))
        log_total = peak_score + jnp.log(lax.optimization_barrier(jnp.sum(jnp.exp(attention_logits - peak_score), axis=-1, keepdims=True)))
        attention_probabilities = jnp.exp(attention_logits - log_total)
        weights_low = lax.optimization_barrier(attention_probabilities.astype(jnp.bfloat16)).astype(jnp.float32)
        attended = jnp.einsum('gjts,sgd->tgjd', weights_low, values).astype(jnp.bfloat16)
        flat_out = attended.reshape(TREE_TOKENS, QUERY_HEADS * HEAD_SIZE)
        attended_wide = lax.optimization_barrier(attended).astype(jnp.float32)
        output_gradient = jnp.dot(upstream, out_weight.T, preferred_element_type=jnp.float32).astype(jnp.bfloat16)
        output_gradient_wide = lax.optimization_barrier(output_gradient).astype(jnp.float32).reshape(TREE_TOKENS, KEY_VALUE_HEADS, queries_per_group, HEAD_SIZE)
        probability_cotangent = jnp.einsum('zpyr,kpr->pyzk', output_gradient_wide, values)
        middle_point = jnp.transpose(lax.optimization_barrier(jnp.sum(output_gradient_wide * attended_wide, axis=-1)), (1, 2, 0))
        logit_cotangent = (attention_probabilities * (probability_cotangent - middle_point[..., None]) * softness_multiplier[None, None, :, None]).astype(jnp.bfloat16)
        logit_cotangent = lax.optimization_barrier(logit_cotangent).astype(jnp.float32)
        query_grad = jnp.einsum('gjts,sgd->tgjd', logit_cotangent, lookup_matrix).astype(jnp.bfloat16)
        key_grad = jnp.einsum('gjts,tgjd->sgd', logit_cotangent, asking_matrix).astype(jnp.bfloat16)
        value_grad = jnp.einsum('gjts,tgjd->sgd', weights_low, output_gradient_wide).astype(jnp.bfloat16)
        gradients = jnp.concatenate([query_grad, key_grad[:, :, None], value_grad[:, :, None]], axis=2)
        return (gradients.reshape(TREE_TOKENS, QKV_W), flat_out)
    gradients, outputs = lax.map(one_tree, (every_row, cot_all, parents, len_all))
    weight_total = jnp.dot(outputs.reshape(ROWS, QUERY_HEADS * HEAD_SIZE).T, cotangent, preferred_element_type=jnp.float32)
    return (gradients.reshape(ROWS, QKV_W), weight_total.astype(jnp.bfloat16))
```

```python
import math

import jax
import jax.numpy as jnp
from jax import lax
from jax.sharding import PartitionSpec as P

QUERY_HEADS = 40
KEY_VALUE_HEADS = 8
HEAD_SIZE = 128
BLK = 128


log_base = 1024.0


def ancestors(parents):
    number = parents.shape[0]
    indices = jnp.arange(number, dtype=jnp.int32)

    def advance(iteration, state):
        current, reached = state
        current = jnp.sum(
            jnp.where(current[:, None] == indices[None, :], parents[None, :], 0), axis=1
        )
        return (current, reached | (current[:, None] == indices[None, :]))

    return lax.fori_loop(0, number, advance, (indices, indices[:, None] == indices[None, :]))[1]


def token_mask(reached, first_row, query_count, key_count):
    query_pos = first_row + jnp.arange(query_count, dtype=jnp.int32)
    key_pos = jnp.arange(key_count, dtype=jnp.int32)
    block_part = reached[first_row // BLK : (first_row + query_count) // BLK, : key_count // BLK]
    expanded = jnp.repeat(jnp.repeat(block_part, BLK, axis=0), BLK, axis=1)
    same_block = (query_pos // BLK)[:, None] == (key_pos // BLK)[None, :]
    return expanded & (jnp.logical_not(same_block) | (key_pos[None, :] <= query_pos[:, None]))


def span_softness(rollout_spans):
    return jnp.log(rollout_spans.astype(jnp.float32)) * (
        1.0 / (math.log(log_base) * math.sqrt(HEAD_SIZE))
    )


def contract_rows(left, right):
    return lax.dot_general(
        left, right, (((0,), (0,)), ((), ())), preferred_element_type=jnp.float32
    )


def contract_cols(left, right):
    return lax.dot_general(
        left, right, (((1,), (1,)), ((), ())), preferred_element_type=jnp.float32
    )


def local(query_key_value_rows, cotangent, out_weight, parents, rollout_spans):
    queries_per_group = QUERY_HEADS // KEY_VALUE_HEADS
    head_rows = lax.all_to_all(query_key_value_rows, "ctx", split_axis=1, concat_axis=0, tiled=True)
    tree_len = head_rows.shape[0]
    kv_local = head_rows.shape[1] // ((queries_per_group + 2) * HEAD_SIZE)
    heads_local = kv_local * queries_per_group
    grouped = head_rows.reshape(tree_len, kv_local, queries_per_group + 2, HEAD_SIZE)
    asking_matrix = grouped[:, :, :queries_per_group]
    lookup_matrix = grouped[:, :, queries_per_group]
    value_rows = grouped[:, :, queries_per_group + 1]
    softness_multiplier = span_softness(rollout_spans)
    reached = ancestors(parents[0])
    block_len = min(512, tree_len)
    block_total = tree_len // block_len
    masks = []
    total_parts = []
    attended_parts = []
    for block_id in range(block_total):
        opening_slot = block_id * block_len
        closing_slot = opening_slot + block_len
        allowed = token_mask(reached, opening_slot, block_len, closing_slot)
        masks.append(allowed)
        attention_logits = jnp.einsum(
            "zpyr,kpr->pyzk",
            asking_matrix[opening_slot:closing_slot],
            lookup_matrix[:closing_slot],
            preferred_element_type=jnp.float32,
        )
        attention_logits = jnp.where(
            allowed[None, None],
            attention_logits * softness_multiplier[opening_slot:closing_slot][None, None, :, None],
            -jnp.inf,
        )
        peak_score = jnp.max(attention_logits, axis=-1, keepdims=True)
        log_total = peak_score + jnp.log(
            jnp.sum(jnp.exp(attention_logits - peak_score), axis=-1, keepdims=True)
        )
        weights_low = jnp.exp(attention_logits - log_total).astype(jnp.bfloat16)
        attended_parts.append(
            jnp.einsum(
                "gjts,sgd->tgjd",
                weights_low,
                value_rows[:closing_slot],
                preferred_element_type=jnp.float32,
            ).astype(jnp.bfloat16)
        )
        total_parts.append(log_total[..., 0])
    attended = jnp.concatenate(attended_parts, axis=0)
    log_totals = jnp.concatenate(total_parts, axis=2)
    flat_out = attended.reshape(tree_len, heads_local * HEAD_SIZE)
    shard_rows = lax.all_gather(cotangent, "ctx", axis=0, tiled=True)
    weight_acc = contract_rows(flat_out, shard_rows)
    local_grad = contract_cols(shard_rows, out_weight).astype(jnp.bfloat16)
    weight_acc, output_gradient = (weight_acc, local_grad)
    weight_part = lax.psum_scatter(weight_acc, "leaf", scatter_dimension=0, tiled=True)
    weight_total = lax.all_gather(weight_part.astype(jnp.bfloat16), "leaf", axis=0, tiled=True)
    key_acc = jnp.zeros((tree_len, kv_local, HEAD_SIZE), jnp.float32)
    value_acc = jnp.zeros((tree_len, kv_local, HEAD_SIZE), jnp.float32)
    query_parts = []
    for head_id in range(heads_local):
        kv_id = head_id // queries_per_group
        inner = head_id % queries_per_group
        query_blocks = []
        for block_id in range(block_total):
            opening_slot = block_id * block_len
            closing_slot = opening_slot + block_len
            query_now = asking_matrix[opening_slot:closing_slot, kv_id, inner]
            keys_now = lookup_matrix[:closing_slot, kv_id]
            values_now = value_rows[:closing_slot, kv_id]
            line_multiplier = softness_multiplier[opening_slot:closing_slot][:, None]
            attention_logits = jnp.where(
                masks[block_id], contract_cols(query_now, keys_now) * line_multiplier, -jnp.inf
            )
            attention_probabilities = jnp.exp(
                attention_logits - log_totals[kv_id, inner, opening_slot:closing_slot][:, None]
            )
            grad_rows = output_gradient[
                opening_slot:closing_slot, head_id * HEAD_SIZE : (head_id + 1) * HEAD_SIZE
            ]
            own_rows = attended[opening_slot:closing_slot, kv_id, inner]
            probability_cotangent = contract_cols(grad_rows, values_now)
            middle_point = jnp.sum(
                grad_rows.astype(jnp.float32) * own_rows.astype(jnp.float32), axis=1
            )
            logit_cotangent = (
                attention_probabilities
                * (probability_cotangent - middle_point[:, None])
                * line_multiplier
            ).astype(jnp.bfloat16)
            query_blocks.append(
                jnp.dot(logit_cotangent, keys_now, preferred_element_type=jnp.float32).astype(
                    jnp.bfloat16
                )
            )
            key_acc = key_acc.at[:closing_slot, kv_id].add(
                contract_rows(logit_cotangent, query_now)
            )
            value_acc = value_acc.at[:closing_slot, kv_id].add(
                contract_rows(attention_probabilities.astype(jnp.bfloat16), grad_rows)
            )
        query_parts.append(jnp.concatenate(query_blocks, axis=0))
    query_grad = jnp.stack(query_parts, axis=1).reshape(
        tree_len, kv_local, queries_per_group, HEAD_SIZE
    )
    gradients = jnp.concatenate(
        [
            query_grad,
            key_acc.astype(jnp.bfloat16)[:, :, None],
            value_acc.astype(jnp.bfloat16)[:, :, None],
        ],
        axis=2,
    )
    gradients = gradients.reshape(tree_len, kv_local * (queries_per_group + 2) * HEAD_SIZE)
    returned = lax.all_to_all(gradients, "ctx", split_axis=0, concat_axis=1, tiled=True)
    return (returned, weight_total)


def solution(mesh):
    placed = (
        P(("leaf", "ctx"), None),
        P(("leaf", "ctx"), None),
        P("ctx", None),
        P("leaf", None),
        P("leaf"),
    )
    return jax.shard_map(
        local,
        mesh=mesh,
        in_specs=placed,
        out_specs=(P(("leaf", "ctx"), None), P("ctx", None)),
        check_vma=False,
    )
```

```python
import math

import jax
import jax.numpy as jnp
from jax import lax
from jax.sharding import PartitionSpec as P

QUERY_HEADS = 40
KEY_VALUE_HEADS = 8
HEAD_SIZE = 128
BLK = 128


log_base = 1024.0


def ancestors(parents):
    number = parents.shape[0]
    indices = jnp.arange(number, dtype=jnp.int32)

    def advance(iteration, state):
        current, reached = state
        current = jnp.sum(
            jnp.where(current[:, None] == indices[None, :], parents[None, :], 0), axis=1
        )
        return (current, reached | (current[:, None] == indices[None, :]))

    return lax.fori_loop(0, number, advance, (indices, indices[:, None] == indices[None, :]))[1]


def token_mask(reached, first_row, query_count, key_count):
    query_pos = first_row + jnp.arange(query_count, dtype=jnp.int32)
    key_pos = jnp.arange(key_count, dtype=jnp.int32)
    block_part = reached[first_row // BLK : (first_row + query_count) // BLK, : key_count // BLK]
    expanded = jnp.repeat(jnp.repeat(block_part, BLK, axis=0), BLK, axis=1)
    same_block = (query_pos // BLK)[:, None] == (key_pos // BLK)[None, :]
    return expanded & (jnp.logical_not(same_block) | (key_pos[None, :] <= query_pos[:, None]))


def span_softness(rollout_spans):
    return jnp.log(rollout_spans.astype(jnp.float32)) * (
        1.0 / (math.log(log_base) * math.sqrt(HEAD_SIZE))
    )


def contract_rows(left, right):
    return lax.dot_general(
        left, right, (((0,), (0,)), ((), ())), preferred_element_type=jnp.float32
    )


def contract_cols(left, right):
    return lax.dot_general(
        left, right, (((1,), (1,)), ((), ())), preferred_element_type=jnp.float32
    )


def local(query_key_value_rows, cotangent, out_weight, parents, rollout_spans):
    queries_per_group = QUERY_HEADS // KEY_VALUE_HEADS
    head_rows = lax.all_to_all(query_key_value_rows, "ctx", split_axis=1, concat_axis=0, tiled=True)
    tree_len = head_rows.shape[0]
    kv_local = head_rows.shape[1] // ((queries_per_group + 2) * HEAD_SIZE)
    heads_local = kv_local * queries_per_group
    grouped = head_rows.reshape(tree_len, kv_local, queries_per_group + 2, HEAD_SIZE)
    asking_matrix = grouped[:, :, :queries_per_group]
    lookup_matrix = grouped[:, :, queries_per_group]
    value_rows = grouped[:, :, queries_per_group + 1]
    softness_multiplier = span_softness(rollout_spans)
    reached = ancestors(parents[0])
    block_len = min(512, tree_len)
    block_total = tree_len // block_len
    masks = []
    total_parts = []
    attended_parts = []
    for block_id in range(block_total):
        opening_slot = block_id * block_len
        closing_slot = opening_slot + block_len
        allowed = token_mask(reached, opening_slot, block_len, closing_slot)
        masks.append(allowed)
        attention_logits = jnp.einsum(
            "zpyr,kpr->pyzk",
            asking_matrix[opening_slot:closing_slot],
            lookup_matrix[:closing_slot],
            preferred_element_type=jnp.float32,
        )
        attention_logits = jnp.where(
            allowed[None, None],
            attention_logits * softness_multiplier[opening_slot:closing_slot][None, None, :, None],
            -jnp.inf,
        )
        peak_score = jnp.max(attention_logits, axis=-1, keepdims=True)
        log_total = peak_score + jnp.log(
            jnp.sum(jnp.exp(attention_logits - peak_score), axis=-1, keepdims=True)
        )
        weights_low = jnp.exp(attention_logits - log_total).astype(jnp.bfloat16)
        attended_parts.append(
            jnp.einsum(
                "gjts,sgd->tgjd",
                weights_low,
                value_rows[:closing_slot],
                preferred_element_type=jnp.float32,
            ).astype(jnp.bfloat16)
        )
        total_parts.append(log_total[..., 0])
    attended = jnp.concatenate(attended_parts, axis=0)
    log_totals = jnp.concatenate(total_parts, axis=2)
    flat_out = attended.reshape(tree_len, heads_local * HEAD_SIZE)
    shard_rows = lax.all_gather(cotangent, "ctx", axis=0, tiled=True)
    weight_acc = contract_rows(flat_out, shard_rows)
    local_grad = contract_cols(shard_rows, out_weight).astype(jnp.bfloat16)
    weight_acc, output_gradient = (weight_acc, local_grad)
    weight_part = lax.psum_scatter(
        weight_acc.astype(jnp.bfloat16), "leaf", scatter_dimension=0, tiled=True
    )
    weight_total = lax.all_gather(weight_part, "leaf", axis=0, tiled=True)
    key_acc = jnp.zeros((tree_len, kv_local, HEAD_SIZE), jnp.float32)
    value_acc = jnp.zeros((tree_len, kv_local, HEAD_SIZE), jnp.float32)
    query_parts = []
    for head_id in range(heads_local):
        kv_id = head_id // queries_per_group
        inner = head_id % queries_per_group
        query_blocks = []
        for block_id in range(block_total):
            opening_slot = block_id * block_len
            closing_slot = opening_slot + block_len
            query_now = asking_matrix[opening_slot:closing_slot, kv_id, inner]
            keys_now = lookup_matrix[:closing_slot, kv_id]
            values_now = value_rows[:closing_slot, kv_id]
            line_multiplier = softness_multiplier[opening_slot:closing_slot][:, None]
            attention_logits = jnp.where(
                masks[block_id], contract_cols(query_now, keys_now) * line_multiplier, -jnp.inf
            )
            attention_probabilities = jnp.exp(
                attention_logits - log_totals[kv_id, inner, opening_slot:closing_slot][:, None]
            )
            grad_rows = output_gradient[
                opening_slot:closing_slot, head_id * HEAD_SIZE : (head_id + 1) * HEAD_SIZE
            ]
            own_rows = attended[opening_slot:closing_slot, kv_id, inner]
            probability_cotangent = contract_cols(grad_rows, values_now)
            middle_point = jnp.sum(
                grad_rows.astype(jnp.float32) * own_rows.astype(jnp.float32), axis=1
            )
            logit_cotangent = (
                attention_probabilities
                * (probability_cotangent - middle_point[:, None])
                * line_multiplier
            ).astype(jnp.bfloat16)
            query_blocks.append(
                jnp.dot(logit_cotangent, keys_now, preferred_element_type=jnp.float32).astype(
                    jnp.bfloat16
                )
            )
            key_acc = key_acc.at[:closing_slot, kv_id].add(
                contract_rows(logit_cotangent, query_now)
            )
            value_acc = value_acc.at[:closing_slot, kv_id].add(
                contract_rows(attention_probabilities.astype(jnp.bfloat16), grad_rows)
            )
        query_parts.append(jnp.concatenate(query_blocks, axis=0))
    query_grad = jnp.stack(query_parts, axis=1).reshape(
        tree_len, kv_local, queries_per_group, HEAD_SIZE
    )
    gradients = jnp.concatenate(
        [
            query_grad,
            key_acc.astype(jnp.bfloat16)[:, :, None],
            value_acc.astype(jnp.bfloat16)[:, :, None],
        ],
        axis=2,
    )
    gradients = gradients.reshape(tree_len, kv_local * (queries_per_group + 2) * HEAD_SIZE)
    returned = lax.all_to_all(gradients, "ctx", split_axis=0, concat_axis=1, tiled=True)
    return (returned, weight_total)


def solution(mesh):
    placed = (
        P(("leaf", "ctx"), None),
        P(("leaf", "ctx"), None),
        P("ctx", None),
        P("leaf", None),
        P("leaf"),
    )
    return jax.shard_map(
        local,
        mesh=mesh,
        in_specs=placed,
        out_specs=(P(("leaf", "ctx"), None), P("ctx", None)),
        check_vma=False,
    )
```

```python
import math

import jax
import jax.numpy as jnp
from jax import lax
from jax.sharding import PartitionSpec as P

QUERY_HEADS = 40
KEY_VALUE_HEADS = 8
HEAD_SIZE = 128
BLK = 128


log_base = 1024.0


def ancestors(parents):
    number = parents.shape[0]
    indices = jnp.arange(number, dtype=jnp.int32)

    def advance(iteration, state):
        current, reached = state
        current = jnp.sum(
            jnp.where(current[:, None] == indices[None, :], parents[None, :], 0), axis=1
        )
        return (current, reached | (current[:, None] == indices[None, :]))

    return lax.fori_loop(0, number, advance, (indices, indices[:, None] == indices[None, :]))[1]


def token_mask(reached, first_row, query_count, key_count):
    query_pos = first_row + jnp.arange(query_count, dtype=jnp.int32)
    key_pos = jnp.arange(key_count, dtype=jnp.int32)
    block_part = reached[first_row // BLK : (first_row + query_count) // BLK, : key_count // BLK]
    expanded = jnp.repeat(jnp.repeat(block_part, BLK, axis=0), BLK, axis=1)
    same_block = (query_pos // BLK)[:, None] == (key_pos // BLK)[None, :]
    return expanded & (jnp.logical_not(same_block) | (key_pos[None, :] <= query_pos[:, None]))


def span_softness(rollout_spans):
    return jnp.log(rollout_spans.astype(jnp.float32)) * (
        1.0 / (math.log(log_base) * math.sqrt(HEAD_SIZE))
    )


def contract_rows(left, right):
    return lax.dot_general(
        left, right, (((0,), (0,)), ((), ())), preferred_element_type=jnp.float32
    )


def contract_cols(left, right):
    return lax.dot_general(
        left, right, (((1,), (1,)), ((), ())), preferred_element_type=jnp.float32
    )


def gather_tree_rows(rows):
    cores = 2
    chips = lax.axis_size("ctx") // cores
    me = lax.axis_index("ctx")
    my_chip = me // cores
    my_core = me % cores
    blocks = [rows]
    chip_of = [my_chip]
    for shift in range(1, chips):
        pairs = [
            (chip * cores + core, ((chip + shift) % chips) * cores + core)
            for chip in range(chips)
            for core in range(cores)
        ]
        blocks.append(lax.ppermute(rows, "ctx", pairs))
        chip_of.append((my_chip - shift) % chips)
    mine = jnp.stack(blocks)
    swap = [(chip * cores + core, chip * cores + 1 - core) for chip in range(chips) for core in range(cores)]
    theirs = lax.ppermute(mine, "ctx", swap)
    block_len = rows.shape[0]
    full = jnp.zeros((chips * cores * block_len, rows.shape[1]), rows.dtype)
    for slot in range(chips):
        for core, source in ((my_core, mine), (1 - my_core, theirs)):
            start = (chip_of[slot] * cores + core) * block_len
            full = lax.dynamic_update_slice(full, source[slot], (start, 0))
    return full


def local(query_key_value_rows, cotangent, out_weight, parents, rollout_spans):
    queries_per_group = QUERY_HEADS // KEY_VALUE_HEADS
    head_rows = lax.all_to_all(query_key_value_rows, "ctx", split_axis=1, concat_axis=0, tiled=True)
    tree_len = head_rows.shape[0]
    kv_local = head_rows.shape[1] // ((queries_per_group + 2) * HEAD_SIZE)
    heads_local = kv_local * queries_per_group
    grouped = head_rows.reshape(tree_len, kv_local, queries_per_group + 2, HEAD_SIZE)
    asking_matrix = grouped[:, :, :queries_per_group]
    lookup_matrix = grouped[:, :, queries_per_group]
    value_rows = grouped[:, :, queries_per_group + 1]
    softness_multiplier = span_softness(rollout_spans)
    reached = ancestors(parents[0])
    block_len = min(512, tree_len)
    block_total = tree_len // block_len
    masks = []
    total_parts = []
    attended_parts = []
    for block_id in range(block_total):
        opening_slot = block_id * block_len
        closing_slot = opening_slot + block_len
        allowed = token_mask(reached, opening_slot, block_len, closing_slot)
        masks.append(allowed)
        attention_logits = jnp.einsum(
            "zpyr,kpr->pyzk",
            asking_matrix[opening_slot:closing_slot],
            lookup_matrix[:closing_slot],
            preferred_element_type=jnp.float32,
        )
        attention_logits = jnp.where(
            allowed[None, None],
            attention_logits * softness_multiplier[opening_slot:closing_slot][None, None, :, None],
            -jnp.inf,
        )
        peak_score = jnp.max(attention_logits, axis=-1, keepdims=True)
        log_total = peak_score + jnp.log(
            jnp.sum(jnp.exp(attention_logits - peak_score), axis=-1, keepdims=True)
        )
        weights_low = jnp.exp(attention_logits - log_total).astype(jnp.bfloat16)
        attended_parts.append(
            jnp.einsum(
                "gjts,sgd->tgjd",
                weights_low,
                value_rows[:closing_slot],
                preferred_element_type=jnp.float32,
            ).astype(jnp.bfloat16)
        )
        total_parts.append(log_total[..., 0])
    attended = jnp.concatenate(attended_parts, axis=0)
    log_totals = jnp.concatenate(total_parts, axis=2)
    flat_out = attended.reshape(tree_len, heads_local * HEAD_SIZE)
    shard_rows = gather_tree_rows(cotangent)
    weight_acc = contract_rows(flat_out, shard_rows)
    local_grad = contract_cols(shard_rows, out_weight).astype(jnp.bfloat16)
    weight_acc, output_gradient = (weight_acc, local_grad)
    weight_part = lax.psum_scatter(
        weight_acc.astype(jnp.bfloat16), "leaf", scatter_dimension=0, tiled=True
    )
    weight_total = lax.all_gather(weight_part, "leaf", axis=0, tiled=True)
    key_acc = jnp.zeros((tree_len, kv_local, HEAD_SIZE), jnp.float32)
    value_acc = jnp.zeros((tree_len, kv_local, HEAD_SIZE), jnp.float32)
    query_parts = []
    for head_id in range(heads_local):
        kv_id = head_id // queries_per_group
        inner = head_id % queries_per_group
        query_blocks = []
        for block_id in range(block_total):
            opening_slot = block_id * block_len
            closing_slot = opening_slot + block_len
            query_now = asking_matrix[opening_slot:closing_slot, kv_id, inner]
            keys_now = lookup_matrix[:closing_slot, kv_id]
            values_now = value_rows[:closing_slot, kv_id]
            line_multiplier = softness_multiplier[opening_slot:closing_slot][:, None]
            attention_logits = jnp.where(
                masks[block_id], contract_cols(query_now, keys_now) * line_multiplier, -jnp.inf
            )
            attention_probabilities = jnp.exp(
                attention_logits - log_totals[kv_id, inner, opening_slot:closing_slot][:, None]
            )
            grad_rows = output_gradient[
                opening_slot:closing_slot, head_id * HEAD_SIZE : (head_id + 1) * HEAD_SIZE
            ]
            own_rows = attended[opening_slot:closing_slot, kv_id, inner]
            probability_cotangent = contract_cols(grad_rows, values_now)
            middle_point = jnp.sum(
                grad_rows.astype(jnp.float32) * own_rows.astype(jnp.float32), axis=1
            )
            logit_cotangent = (
                attention_probabilities
                * (probability_cotangent - middle_point[:, None])
                * line_multiplier
            ).astype(jnp.bfloat16)
            query_blocks.append(
                jnp.dot(logit_cotangent, keys_now, preferred_element_type=jnp.float32).astype(
                    jnp.bfloat16
                )
            )
            key_acc = key_acc.at[:closing_slot, kv_id].add(
                contract_rows(logit_cotangent, query_now)
            )
            value_acc = value_acc.at[:closing_slot, kv_id].add(
                contract_rows(attention_probabilities.astype(jnp.bfloat16), grad_rows)
            )
        query_parts.append(jnp.concatenate(query_blocks, axis=0))
    query_grad = jnp.stack(query_parts, axis=1).reshape(
        tree_len, kv_local, queries_per_group, HEAD_SIZE
    )
    gradients = jnp.concatenate(
        [
            query_grad,
            key_acc.astype(jnp.bfloat16)[:, :, None],
            value_acc.astype(jnp.bfloat16)[:, :, None],
        ],
        axis=2,
    )
    gradients = gradients.reshape(tree_len, kv_local * (queries_per_group + 2) * HEAD_SIZE)
    returned = lax.all_to_all(gradients, "ctx", split_axis=0, concat_axis=1, tiled=True)
    return (returned, weight_total)


def solution(mesh):
    placed = (
        P(("leaf", "ctx"), None),
        P(("leaf", "ctx"), None),
        P("ctx", None),
        P("leaf", None),
        P("leaf"),
    )
    return jax.shard_map(
        local,
        mesh=mesh,
        in_specs=placed,
        out_specs=(P(("leaf", "ctx"), None), P("ctx", None)),
        check_vma=False,
    )
```

```python
import math

import jax
import jax.numpy as jnp
from jax import lax
from jax.sharding import PartitionSpec as P

QUERY_HEADS = 40
KEY_VALUE_HEADS = 8
HEAD_SIZE = 128
BLK = 128


log_base = 1024.0


def ancestors(parents):
    number = parents.shape[0]
    indices = jnp.arange(number, dtype=jnp.int32)

    def advance(iteration, state):
        current, reached = state
        current = jnp.sum(
            jnp.where(current[:, None] == indices[None, :], parents[None, :], 0), axis=1
        )
        return (current, reached | (current[:, None] == indices[None, :]))

    return lax.fori_loop(0, number, advance, (indices, indices[:, None] == indices[None, :]))[1]


def token_mask(reached, first_row, query_count, key_count):
    query_pos = first_row + jnp.arange(query_count, dtype=jnp.int32)
    key_pos = jnp.arange(key_count, dtype=jnp.int32)
    block_part = reached[first_row // BLK : (first_row + query_count) // BLK, : key_count // BLK]
    expanded = jnp.repeat(jnp.repeat(block_part, BLK, axis=0), BLK, axis=1)
    same_block = (query_pos // BLK)[:, None] == (key_pos // BLK)[None, :]
    return expanded & (jnp.logical_not(same_block) | (key_pos[None, :] <= query_pos[:, None]))


def span_softness(rollout_spans):
    return jnp.log(rollout_spans.astype(jnp.float32)) * (
        1.0 / (math.log(log_base) * math.sqrt(HEAD_SIZE))
    )


def contract_rows(left, right):
    return lax.dot_general(
        left, right, (((0,), (0,)), ((), ())), preferred_element_type=jnp.float32
    )


def contract_cols(left, right):
    return lax.dot_general(
        left, right, (((1,), (1,)), ((), ())), preferred_element_type=jnp.float32
    )


def local(query_key_value_rows, cotangent, out_weight, parents, rollout_spans):
    queries_per_group = QUERY_HEADS // KEY_VALUE_HEADS
    head_rows = lax.all_to_all(query_key_value_rows, "ctx", split_axis=1, concat_axis=0, tiled=True)
    tree_len = head_rows.shape[0]
    kv_local = head_rows.shape[1] // ((queries_per_group + 2) * HEAD_SIZE)
    heads_local = kv_local * queries_per_group
    grouped = head_rows.reshape(tree_len, kv_local, queries_per_group + 2, HEAD_SIZE)
    asking_matrix = grouped[:, :, :queries_per_group]
    lookup_matrix = grouped[:, :, queries_per_group]
    value_rows = grouped[:, :, queries_per_group + 1]
    softness_multiplier = span_softness(rollout_spans)
    reached = ancestors(parents[0])
    block_len = min(512, tree_len)
    block_total = tree_len // block_len
    masks = []
    total_parts = []
    attended_parts = []
    for block_id in range(block_total):
        opening_slot = block_id * block_len
        closing_slot = opening_slot + block_len
        allowed = token_mask(reached, opening_slot, block_len, closing_slot)
        masks.append(allowed)
        attention_logits = jnp.einsum(
            "zpyr,kpr->pyzk",
            asking_matrix[opening_slot:closing_slot],
            lookup_matrix[:closing_slot],
            preferred_element_type=jnp.float32,
        )
        attention_logits = jnp.where(
            allowed[None, None],
            attention_logits * softness_multiplier[opening_slot:closing_slot][None, None, :, None],
            -jnp.inf,
        )
        peak_score = jnp.max(attention_logits, axis=-1, keepdims=True)
        log_total = peak_score + jnp.log(
            jnp.sum(jnp.exp(attention_logits - peak_score), axis=-1, keepdims=True)
        )
        weights_low = jnp.exp(attention_logits - log_total).astype(jnp.bfloat16)
        attended_parts.append(
            jnp.einsum(
                "gjts,sgd->tgjd",
                weights_low,
                value_rows[:closing_slot],
                preferred_element_type=jnp.float32,
            ).astype(jnp.bfloat16)
        )
        total_parts.append(log_total[..., 0])
    attended = jnp.concatenate(attended_parts, axis=0)
    log_totals = jnp.concatenate(total_parts, axis=2)
    flat_out = attended.reshape(tree_len, heads_local * HEAD_SIZE)
    shard_rows = lax.all_gather(cotangent, "ctx", axis=0, tiled=True)
    weight_acc = contract_rows(flat_out, shard_rows)
    local_grad = contract_cols(shard_rows, out_weight).astype(jnp.bfloat16)
    weight_acc, output_gradient = (weight_acc, local_grad)
    weight_total = lax.psum(weight_acc.astype(jnp.bfloat16), "leaf")
    key_acc = jnp.zeros((tree_len, kv_local, HEAD_SIZE), jnp.float32)
    value_acc = jnp.zeros((tree_len, kv_local, HEAD_SIZE), jnp.float32)
    query_parts = []
    for head_id in range(heads_local):
        kv_id = head_id // queries_per_group
        inner = head_id % queries_per_group
        query_blocks = []
        for block_id in range(block_total):
            opening_slot = block_id * block_len
            closing_slot = opening_slot + block_len
            query_now = asking_matrix[opening_slot:closing_slot, kv_id, inner]
            keys_now = lookup_matrix[:closing_slot, kv_id]
            values_now = value_rows[:closing_slot, kv_id]
            line_multiplier = softness_multiplier[opening_slot:closing_slot][:, None]
            attention_logits = jnp.where(
                masks[block_id], contract_cols(query_now, keys_now) * line_multiplier, -jnp.inf
            )
            attention_probabilities = jnp.exp(
                attention_logits - log_totals[kv_id, inner, opening_slot:closing_slot][:, None]
            )
            grad_rows = output_gradient[
                opening_slot:closing_slot, head_id * HEAD_SIZE : (head_id + 1) * HEAD_SIZE
            ]
            own_rows = attended[opening_slot:closing_slot, kv_id, inner]
            probability_cotangent = contract_cols(grad_rows, values_now)
            middle_point = jnp.sum(
                grad_rows.astype(jnp.float32) * own_rows.astype(jnp.float32), axis=1
            )
            logit_cotangent = (
                attention_probabilities
                * (probability_cotangent - middle_point[:, None])
                * line_multiplier
            ).astype(jnp.bfloat16)
            query_blocks.append(
                jnp.dot(logit_cotangent, keys_now, preferred_element_type=jnp.float32).astype(
                    jnp.bfloat16
                )
            )
            key_acc = key_acc.at[:closing_slot, kv_id].add(
                contract_rows(logit_cotangent, query_now)
            )
            value_acc = value_acc.at[:closing_slot, kv_id].add(
                contract_rows(attention_probabilities.astype(jnp.bfloat16), grad_rows)
            )
        query_parts.append(jnp.concatenate(query_blocks, axis=0))
    query_grad = jnp.stack(query_parts, axis=1).reshape(
        tree_len, kv_local, queries_per_group, HEAD_SIZE
    )
    gradients = jnp.concatenate(
        [
            query_grad,
            key_acc.astype(jnp.bfloat16)[:, :, None],
            value_acc.astype(jnp.bfloat16)[:, :, None],
        ],
        axis=2,
    )
    gradients = gradients.reshape(tree_len, kv_local * (queries_per_group + 2) * HEAD_SIZE)
    returned = lax.all_to_all(gradients, "ctx", split_axis=0, concat_axis=1, tiled=True)
    return (returned, weight_total)


def solution(mesh):
    placed = (
        P(("leaf", "ctx"), None),
        P(("leaf", "ctx"), None),
        P("ctx", None),
        P("leaf", None),
        P("leaf"),
    )
    return jax.shard_map(
        local,
        mesh=mesh,
        in_specs=placed,
        out_specs=(P(("leaf", "ctx"), None), P("ctx", None)),
        check_vma=False,
    )
```

```python
import math

import jax
import jax.numpy as jnp
from jax import lax
from jax.sharding import PartitionSpec as P

QUERY_HEADS = 40
KEY_VALUE_HEADS = 8
HEAD_SIZE = 128
BLK = 128


log_base = 1024.0


def ancestors(parents):
    number = parents.shape[0]
    indices = jnp.arange(number, dtype=jnp.int32)

    def advance(iteration, state):
        current, reached = state
        current = jnp.sum(
            jnp.where(current[:, None] == indices[None, :], parents[None, :], 0), axis=1
        )
        return (current, reached | (current[:, None] == indices[None, :]))

    return lax.fori_loop(0, number, advance, (indices, indices[:, None] == indices[None, :]))[1]


def token_mask(reached, first_row, query_count, key_count):
    query_pos = first_row + jnp.arange(query_count, dtype=jnp.int32)
    key_pos = jnp.arange(key_count, dtype=jnp.int32)
    block_part = reached[first_row // BLK : (first_row + query_count) // BLK, : key_count // BLK]
    expanded = jnp.repeat(jnp.repeat(block_part, BLK, axis=0), BLK, axis=1)
    same_block = (query_pos // BLK)[:, None] == (key_pos // BLK)[None, :]
    return expanded & (jnp.logical_not(same_block) | (key_pos[None, :] <= query_pos[:, None]))


def span_softness(rollout_spans):
    return jnp.log(rollout_spans.astype(jnp.float32)) * (
        1.0 / (math.log(log_base) * math.sqrt(HEAD_SIZE))
    )


def contract_rows(left, right):
    return lax.dot_general(
        left, right, (((0,), (0,)), ((), ())), preferred_element_type=jnp.float32
    )


def contract_cols(left, right):
    return lax.dot_general(
        left, right, (((1,), (1,)), ((), ())), preferred_element_type=jnp.float32
    )


def local(query_key_value_rows, cotangent, out_weight, parents, rollout_spans):
    queries_per_group = QUERY_HEADS // KEY_VALUE_HEADS
    head_rows = lax.all_to_all(query_key_value_rows, "ctx", split_axis=1, concat_axis=0, tiled=True)
    tree_len = head_rows.shape[0]
    kv_local = head_rows.shape[1] // ((queries_per_group + 2) * HEAD_SIZE)
    heads_local = kv_local * queries_per_group
    grouped = head_rows.reshape(tree_len, kv_local, queries_per_group + 2, HEAD_SIZE)
    asking_matrix = grouped[:, :, :queries_per_group]
    lookup_matrix = grouped[:, :, queries_per_group]
    value_rows = grouped[:, :, queries_per_group + 1]
    softness_multiplier = span_softness(rollout_spans)
    reached = ancestors(parents[0])
    block_len = min(512, tree_len)
    block_total = tree_len // block_len
    masks = []
    total_parts = []
    attended_parts = []
    for block_id in range(block_total):
        opening_slot = block_id * block_len
        closing_slot = opening_slot + block_len
        allowed = token_mask(reached, opening_slot, block_len, closing_slot)
        masks.append(allowed)
        attention_logits = jnp.einsum(
            "zpyr,kpr->pyzk",
            asking_matrix[opening_slot:closing_slot],
            lookup_matrix[:closing_slot],
            preferred_element_type=jnp.float32,
        )
        attention_logits = jnp.where(
            allowed[None, None],
            attention_logits * softness_multiplier[opening_slot:closing_slot][None, None, :, None],
            -jnp.inf,
        )
        peak_score = jnp.max(attention_logits, axis=-1, keepdims=True)
        log_total = peak_score + jnp.log(
            jnp.sum(jnp.exp(attention_logits - peak_score), axis=-1, keepdims=True)
        )
        weights_low = jnp.exp(attention_logits - log_total).astype(jnp.bfloat16)
        attended_parts.append(
            jnp.einsum(
                "gjts,sgd->tgjd",
                weights_low,
                value_rows[:closing_slot],
                preferred_element_type=jnp.float32,
            ).astype(jnp.bfloat16)
        )
        total_parts.append(log_total[..., 0])
    attended = jnp.concatenate(attended_parts, axis=0)
    log_totals = jnp.concatenate(total_parts, axis=2)
    flat_out = attended.reshape(tree_len, heads_local * HEAD_SIZE)
    shard_rows = lax.all_gather(cotangent, "ctx", axis=0, tiled=True)
    weight_low = contract_rows(flat_out, shard_rows).astype(jnp.bfloat16)
    weight_low, shard_rows = lax.optimization_barrier((weight_low, shard_rows))
    weight_total = lax.psum(weight_low, "leaf")
    def backward_part():
        output_gradient = contract_cols(shard_rows, out_weight).astype(jnp.bfloat16)
        key_acc = jnp.zeros((tree_len, kv_local, HEAD_SIZE), jnp.float32)
        value_acc = jnp.zeros((tree_len, kv_local, HEAD_SIZE), jnp.float32)
        query_parts = []
        for head_id in range(heads_local):
            kv_id = head_id // queries_per_group
            inner = head_id % queries_per_group
            query_blocks = []
            for block_id in range(block_total):
                opening_slot = block_id * block_len
                closing_slot = opening_slot + block_len
                query_now = asking_matrix[opening_slot:closing_slot, kv_id, inner]
                keys_now = lookup_matrix[:closing_slot, kv_id]
                values_now = value_rows[:closing_slot, kv_id]
                line_multiplier = softness_multiplier[opening_slot:closing_slot][:, None]
                attention_logits = jnp.where(
                    masks[block_id], contract_cols(query_now, keys_now) * line_multiplier, -jnp.inf
                )
                attention_probabilities = jnp.exp(
                    attention_logits - log_totals[kv_id, inner, opening_slot:closing_slot][:, None]
                )
                grad_rows = output_gradient[
                    opening_slot:closing_slot, head_id * HEAD_SIZE : (head_id + 1) * HEAD_SIZE
                ]
                own_rows = attended[opening_slot:closing_slot, kv_id, inner]
                probability_cotangent = contract_cols(grad_rows, values_now)
                middle_point = jnp.sum(
                    grad_rows.astype(jnp.float32) * own_rows.astype(jnp.float32), axis=1
                )
                logit_cotangent = (
                    attention_probabilities
                    * (probability_cotangent - middle_point[:, None])
                    * line_multiplier
                ).astype(jnp.bfloat16)
                query_blocks.append(
                    jnp.dot(logit_cotangent, keys_now, preferred_element_type=jnp.float32).astype(
                        jnp.bfloat16
                    )
                )
                key_acc = key_acc.at[:closing_slot, kv_id].add(
                    contract_rows(logit_cotangent, query_now)
                )
                value_acc = value_acc.at[:closing_slot, kv_id].add(
                    contract_rows(attention_probabilities.astype(jnp.bfloat16), grad_rows)
                )
            query_parts.append(jnp.concatenate(query_blocks, axis=0))
        query_grad = jnp.stack(query_parts, axis=1).reshape(
            tree_len, kv_local, queries_per_group, HEAD_SIZE
        )
        gradients = jnp.concatenate(
            [
                query_grad,
                key_acc.astype(jnp.bfloat16)[:, :, None],
                value_acc.astype(jnp.bfloat16)[:, :, None],
            ],
            axis=2,
        )
        gradients = gradients.reshape(tree_len, kv_local * (queries_per_group + 2) * HEAD_SIZE)
        return gradients

    def no_part():
        return jnp.zeros((tree_len, kv_local * (queries_per_group + 2) * HEAD_SIZE), jnp.bfloat16)

    gradients = lax.cond(lax.axis_index("ctx") >= 0, backward_part, no_part)
    returned = lax.all_to_all(gradients, "ctx", split_axis=0, concat_axis=1, tiled=True)
    return (returned, weight_total)


def solution(mesh):
    placed = (
        P(("leaf", "ctx"), None),
        P(("leaf", "ctx"), None),
        P("ctx", None),
        P("leaf", None),
        P("leaf"),
    )
    return jax.shard_map(
        local,
        mesh=mesh,
        in_specs=placed,
        out_specs=(P(("leaf", "ctx"), None), P("ctx", None)),
        check_vma=False,
    )
```

```python
import math

import jax
import jax.numpy as jnp
from jax import lax
from jax.sharding import PartitionSpec as P

QUERY_HEADS = 40
KEY_VALUE_HEADS = 8
HEAD_SIZE = 128
BLK = 128


log_base = 1024.0
CTX = ("x", "core")


def ancestors(parents):
    number = parents.shape[0]
    indices = jnp.arange(number, dtype=jnp.int32)

    def advance(iteration, state):
        current, reached = state
        current = jnp.sum(
            jnp.where(current[:, None] == indices[None, :], parents[None, :], 0), axis=1
        )
        return (current, reached | (current[:, None] == indices[None, :]))

    return lax.fori_loop(0, number, advance, (indices, indices[:, None] == indices[None, :]))[1]


def token_mask(reached, first_row, query_count, key_count):
    query_pos = first_row + jnp.arange(query_count, dtype=jnp.int32)
    key_pos = jnp.arange(key_count, dtype=jnp.int32)
    block_part = reached[first_row // BLK : (first_row + query_count) // BLK, : key_count // BLK]
    expanded = jnp.repeat(jnp.repeat(block_part, BLK, axis=0), BLK, axis=1)
    same_block = (query_pos // BLK)[:, None] == (key_pos // BLK)[None, :]
    return expanded & (jnp.logical_not(same_block) | (key_pos[None, :] <= query_pos[:, None]))


def span_softness(rollout_spans):
    return jnp.log(rollout_spans.astype(jnp.float32)) * (
        1.0 / (math.log(log_base) * math.sqrt(HEAD_SIZE))
    )


def contract_rows(left, right):
    return lax.dot_general(
        left, right, (((0,), (0,)), ((), ())), preferred_element_type=jnp.float32
    )


def contract_cols(left, right):
    return lax.dot_general(
        left, right, (((1,), (1,)), ((), ())), preferred_element_type=jnp.float32
    )


def local(query_key_value_rows, cotangent, out_weight, parents, rollout_spans):
    queries_per_group = QUERY_HEADS // KEY_VALUE_HEADS
    head_rows = lax.all_to_all(query_key_value_rows, CTX, split_axis=1, concat_axis=0, tiled=True)
    tree_len = head_rows.shape[0]
    kv_local = head_rows.shape[1] // ((queries_per_group + 2) * HEAD_SIZE)
    heads_local = kv_local * queries_per_group
    grouped = head_rows.reshape(tree_len, kv_local, queries_per_group + 2, HEAD_SIZE)
    asking_matrix = grouped[:, :, :queries_per_group]
    lookup_matrix = grouped[:, :, queries_per_group]
    value_rows = grouped[:, :, queries_per_group + 1]
    softness_multiplier = span_softness(rollout_spans)
    reached = ancestors(parents[0])
    block_len = min(512, tree_len)
    block_total = tree_len // block_len
    masks = []
    total_parts = []
    attended_parts = []
    for block_id in range(block_total):
        opening_slot = block_id * block_len
        closing_slot = opening_slot + block_len
        allowed = token_mask(reached, opening_slot, block_len, closing_slot)
        masks.append(allowed)
        attention_logits = jnp.einsum(
            "zpyr,kpr->pyzk",
            asking_matrix[opening_slot:closing_slot],
            lookup_matrix[:closing_slot],
            preferred_element_type=jnp.float32,
        )
        attention_logits = jnp.where(
            allowed[None, None],
            attention_logits * softness_multiplier[opening_slot:closing_slot][None, None, :, None],
            -jnp.inf,
        )
        peak_score = jnp.max(attention_logits, axis=-1, keepdims=True)
        log_total = peak_score + jnp.log(
            jnp.sum(jnp.exp(attention_logits - peak_score), axis=-1, keepdims=True)
        )
        weights_low = jnp.exp(attention_logits - log_total).astype(jnp.bfloat16)
        attended_parts.append(
            jnp.einsum(
                "gjts,sgd->tgjd",
                weights_low,
                value_rows[:closing_slot],
                preferred_element_type=jnp.float32,
            ).astype(jnp.bfloat16)
        )
        total_parts.append(log_total[..., 0])
    attended = jnp.concatenate(attended_parts, axis=0)
    log_totals = jnp.concatenate(total_parts, axis=2)
    flat_out = attended.reshape(tree_len, heads_local * HEAD_SIZE)
    same_rows = lax.all_gather(cotangent, "x", axis=0, tiled=True)
    sibling_rows = lax.ppermute(same_rows, "core", [(0, 1), (1, 0)])
    core_id = lax.axis_index("core")
    chips = lax.axis_size("x")
    row_block = cotangent.shape[0]
    out_blocks = flat_out.reshape(chips, 2, row_block, flat_out.shape[1])
    attended_same = lax.dynamic_index_in_dim(out_blocks, core_id, axis=1, keepdims=False)
    attended_sibling = lax.dynamic_index_in_dim(out_blocks, 1 - core_id, axis=1, keepdims=False)
    weight_low = (
        contract_rows(attended_same.reshape(-1, flat_out.shape[1]), same_rows)
        + contract_rows(attended_sibling.reshape(-1, flat_out.shape[1]), sibling_rows)
    ).astype(jnp.bfloat16)
    weight_low, same_rows, sibling_rows = lax.optimization_barrier(
        (weight_low, same_rows, sibling_rows)
    )
    weight_total = lax.psum(weight_low, "leaf")
    def backward_part():
        grad_same = contract_cols(same_rows, out_weight).astype(jnp.bfloat16)
        grad_sibling = contract_cols(sibling_rows, out_weight).astype(jnp.bfloat16)
        first_core = core_id == 0
        grad_even = jnp.where(first_core, grad_same, grad_sibling)
        grad_odd = jnp.where(first_core, grad_sibling, grad_same)
        output_gradient = jnp.stack(
            [grad_even.reshape(chips, row_block, -1), grad_odd.reshape(chips, row_block, -1)],
            axis=1,
        ).reshape(tree_len, -1)
        key_acc = jnp.zeros((tree_len, kv_local, HEAD_SIZE), jnp.float32)
        value_acc = jnp.zeros((tree_len, kv_local, HEAD_SIZE), jnp.float32)
        query_parts = []
        for head_id in range(heads_local):
            kv_id = head_id // queries_per_group
            inner = head_id % queries_per_group
            query_blocks = []
            for block_id in range(block_total):
                opening_slot = block_id * block_len
                closing_slot = opening_slot + block_len
                query_now = asking_matrix[opening_slot:closing_slot, kv_id, inner]
                keys_now = lookup_matrix[:closing_slot, kv_id]
                values_now = value_rows[:closing_slot, kv_id]
                line_multiplier = softness_multiplier[opening_slot:closing_slot][:, None]
                attention_logits = jnp.where(
                    masks[block_id], contract_cols(query_now, keys_now) * line_multiplier, -jnp.inf
                )
                attention_probabilities = jnp.exp(
                    attention_logits - log_totals[kv_id, inner, opening_slot:closing_slot][:, None]
                )
                grad_rows = output_gradient[
                    opening_slot:closing_slot, head_id * HEAD_SIZE : (head_id + 1) * HEAD_SIZE
                ]
                own_rows = attended[opening_slot:closing_slot, kv_id, inner]
                probability_cotangent = contract_cols(grad_rows, values_now)
                middle_point = jnp.sum(
                    grad_rows.astype(jnp.float32) * own_rows.astype(jnp.float32), axis=1
                )
                logit_cotangent = (
                    attention_probabilities
                    * (probability_cotangent - middle_point[:, None])
                    * line_multiplier
                ).astype(jnp.bfloat16)
                query_blocks.append(
                    jnp.dot(logit_cotangent, keys_now, preferred_element_type=jnp.float32).astype(
                        jnp.bfloat16
                    )
                )
                key_acc = key_acc.at[:closing_slot, kv_id].add(
                    contract_rows(logit_cotangent, query_now)
                )
                value_acc = value_acc.at[:closing_slot, kv_id].add(
                    contract_rows(attention_probabilities.astype(jnp.bfloat16), grad_rows)
                )
            query_parts.append(jnp.concatenate(query_blocks, axis=0))
        query_grad = jnp.stack(query_parts, axis=1).reshape(
            tree_len, kv_local, queries_per_group, HEAD_SIZE
        )
        gradients = jnp.concatenate(
            [
                query_grad,
                key_acc.astype(jnp.bfloat16)[:, :, None],
                value_acc.astype(jnp.bfloat16)[:, :, None],
            ],
            axis=2,
        )
        gradients = gradients.reshape(tree_len, kv_local * (queries_per_group + 2) * HEAD_SIZE)
        return gradients

    def no_part():
        return jnp.zeros((tree_len, kv_local * (queries_per_group + 2) * HEAD_SIZE), jnp.bfloat16)

    gradients = lax.cond(core_id >= 0, backward_part, no_part)
    returned = lax.all_to_all(gradients, CTX, split_axis=0, concat_axis=1, tiled=True)
    return (returned, weight_total)


def solution(mesh):
    cores = 2
    split = jax.sharding.Mesh(
        mesh.devices.reshape(mesh.shape["leaf"], mesh.shape["ctx"] // cores, cores),
        ("leaf",) + CTX,
    )
    placed = (
        P(("leaf",) + CTX, None),
        P(("leaf",) + CTX, None),
        P(CTX, None),
        P("leaf", None),
        P("leaf"),
    )
    return jax.shard_map(
        local,
        mesh=split,
        in_specs=placed,
        out_specs=(P(("leaf",) + CTX, None), P(CTX, None)),
        check_vma=False,
    )
```

```python
import math

import jax
import jax.numpy as jnp
from jax import lax
from jax.sharding import PartitionSpec as P

QUERY_HEADS = 40
KEY_VALUE_HEADS = 8
HEAD_SIZE = 128
BLK = 128


log_base = 1024.0


def ancestors(parents):
    number = parents.shape[0]
    indices = jnp.arange(number, dtype=jnp.int32)

    def advance(iteration, state):
        current, reached = state
        current = jnp.sum(
            jnp.where(current[:, None] == indices[None, :], parents[None, :], 0), axis=1
        )
        return (current, reached | (current[:, None] == indices[None, :]))

    return lax.fori_loop(0, number, advance, (indices, indices[:, None] == indices[None, :]))[1]


def token_mask(reached, first_row, query_count, key_count):
    query_pos = first_row + jnp.arange(query_count, dtype=jnp.int32)
    key_pos = jnp.arange(key_count, dtype=jnp.int32)
    block_part = reached[first_row // BLK : (first_row + query_count) // BLK, : key_count // BLK]
    expanded = jnp.repeat(jnp.repeat(block_part, BLK, axis=0), BLK, axis=1)
    same_block = (query_pos // BLK)[:, None] == (key_pos // BLK)[None, :]
    return expanded & (jnp.logical_not(same_block) | (key_pos[None, :] <= query_pos[:, None]))


def span_softness(rollout_spans):
    return jnp.log(rollout_spans.astype(jnp.float32)) * (
        1.0 / (math.log(log_base) * math.sqrt(HEAD_SIZE))
    )


def contract_rows(left, right):
    return lax.dot_general(
        left, right, (((0,), (0,)), ((), ())), preferred_element_type=jnp.float32
    )


def contract_cols(left, right):
    return lax.dot_general(
        left, right, (((1,), (1,)), ((), ())), preferred_element_type=jnp.float32
    )


def local(query_key_value_rows, cotangent, out_weight, parents, rollout_spans):
    queries_per_group = QUERY_HEADS // KEY_VALUE_HEADS
    head_rows = lax.all_to_all(query_key_value_rows, "ctx", split_axis=1, concat_axis=0, tiled=True)
    tree_len = head_rows.shape[0]
    kv_local = head_rows.shape[1] // ((queries_per_group + 2) * HEAD_SIZE)
    heads_local = kv_local * queries_per_group
    grouped = head_rows.reshape(tree_len, kv_local, queries_per_group + 2, HEAD_SIZE)
    asking_matrix = grouped[:, :, :queries_per_group]
    lookup_matrix = grouped[:, :, queries_per_group]
    value_rows = grouped[:, :, queries_per_group + 1]
    softness_multiplier = span_softness(rollout_spans)
    reached = ancestors(parents[0])
    block_len = min(512, tree_len)
    block_total = tree_len // block_len
    masks = []
    total_parts = []
    attended_parts = []
    for block_id in range(block_total):
        opening_slot = block_id * block_len
        closing_slot = opening_slot + block_len
        allowed = token_mask(reached, opening_slot, block_len, closing_slot)
        masks.append(allowed)
        attention_logits = jnp.einsum(
            "zpyr,kpr->pyzk",
            asking_matrix[opening_slot:closing_slot],
            lookup_matrix[:closing_slot],
            preferred_element_type=jnp.float32,
        )
        attention_logits = jnp.where(
            allowed[None, None],
            attention_logits * softness_multiplier[opening_slot:closing_slot][None, None, :, None],
            -jnp.inf,
        )
        peak_score = jnp.max(attention_logits, axis=-1, keepdims=True)
        log_total = peak_score + jnp.log(
            jnp.sum(jnp.exp(attention_logits - peak_score), axis=-1, keepdims=True)
        )
        weights_low = jnp.exp(attention_logits - log_total).astype(jnp.bfloat16)
        attended_parts.append(
            jnp.einsum(
                "gjts,sgd->tgjd",
                weights_low,
                value_rows[:closing_slot],
                preferred_element_type=jnp.float32,
            ).astype(jnp.bfloat16)
        )
        total_parts.append(log_total[..., 0])
    attended = jnp.concatenate(attended_parts, axis=0)
    log_totals = jnp.concatenate(total_parts, axis=2)
    flat_out = attended.reshape(tree_len, heads_local * HEAD_SIZE)
    shard_rows = lax.all_gather(cotangent, "ctx", axis=0, tiled=True)
    weight_low = contract_rows(flat_out, shard_rows).astype(jnp.bfloat16)
    weight_low, shard_rows = lax.optimization_barrier((weight_low, shard_rows))
    weight_total = lax.psum(weight_low, "leaf")
    def backward_part():
        output_gradient = contract_cols(shard_rows, out_weight).astype(jnp.bfloat16)
        asking_heads = asking_matrix.reshape(tree_len, heads_local, HEAD_SIZE)
        attended_heads = attended.reshape(tree_len, heads_local, HEAD_SIZE)
        grad_heads = output_gradient.reshape(tree_len, heads_local, HEAD_SIZE)
        totals_heads = log_totals.reshape(heads_local, tree_len)

        def one_head(head_id, carry):
            key_acc, value_acc, query_grad = carry
            kv_id = head_id // queries_per_group
            keys_all = lax.dynamic_index_in_dim(lookup_matrix, kv_id, axis=1, keepdims=False)
            values_all = lax.dynamic_index_in_dim(value_rows, kv_id, axis=1, keepdims=False)
            query_all = lax.dynamic_index_in_dim(asking_heads, head_id, axis=1, keepdims=False)
            grad_all = lax.dynamic_index_in_dim(grad_heads, head_id, axis=1, keepdims=False)
            own_all = lax.dynamic_index_in_dim(attended_heads, head_id, axis=1, keepdims=False)
            totals_all = lax.dynamic_index_in_dim(totals_heads, head_id, axis=0, keepdims=False)
            key_now = lax.dynamic_index_in_dim(key_acc, kv_id, axis=1, keepdims=False)
            value_now = lax.dynamic_index_in_dim(value_acc, kv_id, axis=1, keepdims=False)
            query_blocks = []
            for block_id in range(block_total):
                opening_slot = block_id * block_len
                closing_slot = opening_slot + block_len
                query_now = query_all[opening_slot:closing_slot]
                keys_now = keys_all[:closing_slot]
                values_now = values_all[:closing_slot]
                line_multiplier = softness_multiplier[opening_slot:closing_slot][:, None]
                attention_logits = jnp.where(
                    masks[block_id], contract_cols(query_now, keys_now) * line_multiplier, -jnp.inf
                )
                attention_probabilities = jnp.exp(
                    attention_logits - totals_all[opening_slot:closing_slot][:, None]
                )
                grad_rows = grad_all[opening_slot:closing_slot]
                own_rows = own_all[opening_slot:closing_slot]
                probability_cotangent = contract_cols(grad_rows, values_now)
                middle_point = jnp.sum(
                    grad_rows.astype(jnp.float32) * own_rows.astype(jnp.float32), axis=1
                )
                logit_cotangent = (
                    attention_probabilities
                    * (probability_cotangent - middle_point[:, None])
                    * line_multiplier
                ).astype(jnp.bfloat16)
                query_blocks.append(
                    jnp.dot(logit_cotangent, keys_now, preferred_element_type=jnp.float32).astype(
                        jnp.bfloat16
                    )
                )
                key_now = key_now.at[:closing_slot].add(contract_rows(logit_cotangent, query_now))
                value_now = value_now.at[:closing_slot].add(
                    contract_rows(attention_probabilities.astype(jnp.bfloat16), grad_rows)
                )
            key_acc = lax.dynamic_update_index_in_dim(key_acc, key_now, kv_id, axis=1)
            value_acc = lax.dynamic_update_index_in_dim(value_acc, value_now, kv_id, axis=1)
            query_grad = lax.dynamic_update_index_in_dim(
                query_grad, jnp.concatenate(query_blocks, axis=0), head_id, axis=1
            )
            return key_acc, value_acc, query_grad

        key_acc, value_acc, query_grad = lax.fori_loop(
            0,
            heads_local,
            one_head,
            (
                jnp.zeros((tree_len, kv_local, HEAD_SIZE), jnp.float32),
                jnp.zeros((tree_len, kv_local, HEAD_SIZE), jnp.float32),
                jnp.zeros((tree_len, heads_local, HEAD_SIZE), jnp.bfloat16),
            ),
        )
        query_grad = query_grad.reshape(tree_len, kv_local, queries_per_group, HEAD_SIZE)
        gradients = jnp.concatenate(
            [
                query_grad,
                key_acc.astype(jnp.bfloat16)[:, :, None],
                value_acc.astype(jnp.bfloat16)[:, :, None],
            ],
            axis=2,
        )
        gradients = gradients.reshape(tree_len, kv_local * (queries_per_group + 2) * HEAD_SIZE)
        return gradients

    def no_part():
        return jnp.zeros((tree_len, kv_local * (queries_per_group + 2) * HEAD_SIZE), jnp.bfloat16)

    gradients = lax.cond(lax.axis_index("ctx") >= 0, backward_part, no_part)
    returned = lax.all_to_all(gradients, "ctx", split_axis=0, concat_axis=1, tiled=True)
    return (returned, weight_total)


def solution(mesh):
    placed = (
        P(("leaf", "ctx"), None),
        P(("leaf", "ctx"), None),
        P("ctx", None),
        P("leaf", None),
        P("leaf"),
    )
    return jax.shard_map(
        local,
        mesh=mesh,
        in_specs=placed,
        out_specs=(P(("leaf", "ctx"), None), P("ctx", None)),
        check_vma=False,
    )
```

```python
import math

import jax
import jax.numpy as jnp
from jax import lax
from jax.sharding import PartitionSpec as P

QUERY_HEADS = 40
KEY_VALUE_HEADS = 8
HEAD_SIZE = 128
BLK = 128


log_base = 1024.0


def ancestors(parents):
    number = parents.shape[0]
    indices = jnp.arange(number, dtype=jnp.int32)

    def advance(iteration, state):
        current, reached = state
        current = jnp.sum(
            jnp.where(current[:, None] == indices[None, :], parents[None, :], 0), axis=1
        )
        return (current, reached | (current[:, None] == indices[None, :]))

    return lax.fori_loop(0, number, advance, (indices, indices[:, None] == indices[None, :]))[1]


def token_mask(reached, first_row, query_count, key_count):
    query_pos = first_row + jnp.arange(query_count, dtype=jnp.int32)
    key_pos = jnp.arange(key_count, dtype=jnp.int32)
    block_part = reached[first_row // BLK : (first_row + query_count) // BLK, : key_count // BLK]
    expanded = jnp.repeat(jnp.repeat(block_part, BLK, axis=0), BLK, axis=1)
    same_block = (query_pos // BLK)[:, None] == (key_pos // BLK)[None, :]
    return expanded & (jnp.logical_not(same_block) | (key_pos[None, :] <= query_pos[:, None]))


def span_softness(rollout_spans):
    return jnp.log(rollout_spans.astype(jnp.float32)) * (
        1.0 / (math.log(log_base) * math.sqrt(HEAD_SIZE))
    )


def contract_rows(left, right):
    return lax.dot_general(
        left, right, (((0,), (0,)), ((), ())), preferred_element_type=jnp.float32
    )


def contract_cols(left, right):
    return lax.dot_general(
        left, right, (((1,), (1,)), ((), ())), preferred_element_type=jnp.float32
    )


def local(query_key_value_rows, cotangent, out_weight, parents, rollout_spans):
    queries_per_group = QUERY_HEADS // KEY_VALUE_HEADS
    head_rows = lax.all_to_all(query_key_value_rows, "ctx", split_axis=1, concat_axis=0, tiled=True)
    tree_len = head_rows.shape[0]
    kv_local = head_rows.shape[1] // ((queries_per_group + 2) * HEAD_SIZE)
    heads_local = kv_local * queries_per_group
    grouped = head_rows.reshape(tree_len, kv_local, queries_per_group + 2, HEAD_SIZE)
    asking_matrix = grouped[:, :, :queries_per_group]
    lookup_matrix = grouped[:, :, queries_per_group]
    value_rows = grouped[:, :, queries_per_group + 1]
    softness_multiplier = span_softness(rollout_spans)
    reached = ancestors(parents[0])
    block_len = min(512, tree_len)
    block_total = tree_len // block_len
    masks = []
    total_parts = []
    attended_parts = []
    for block_id in range(block_total):
        opening_slot = block_id * block_len
        closing_slot = opening_slot + block_len
        allowed = token_mask(reached, opening_slot, block_len, closing_slot)
        masks.append(allowed)
        attention_logits = jnp.einsum(
            "zpyr,kpr->pyzk",
            asking_matrix[opening_slot:closing_slot],
            lookup_matrix[:closing_slot],
            preferred_element_type=jnp.float32,
        )
        attention_logits = jnp.where(
            allowed[None, None],
            attention_logits * softness_multiplier[opening_slot:closing_slot][None, None, :, None],
            -jnp.inf,
        )
        peak_score = jnp.max(attention_logits, axis=-1, keepdims=True)
        log_total = peak_score + jnp.log(
            jnp.sum(jnp.exp(attention_logits - peak_score), axis=-1, keepdims=True)
        )
        weights_low = jnp.exp(attention_logits - log_total).astype(jnp.bfloat16)
        attended_parts.append(
            jnp.einsum(
                "gjts,sgd->tgjd",
                weights_low,
                value_rows[:closing_slot],
                preferred_element_type=jnp.float32,
            ).astype(jnp.bfloat16)
        )
        total_parts.append(log_total[..., 0])
    attended = jnp.concatenate(attended_parts, axis=0)
    log_totals = jnp.concatenate(total_parts, axis=2)
    flat_out = attended.reshape(tree_len, heads_local * HEAD_SIZE)
    ctx_size = lax.axis_size("ctx")
    shard_rows = lax.all_to_all(
        jnp.tile(cotangent, (ctx_size, 1)), "ctx", split_axis=0, concat_axis=0, tiled=True
    )
    weight_low = contract_rows(flat_out, shard_rows).astype(jnp.bfloat16)
    weight_low, shard_rows = lax.optimization_barrier((weight_low, shard_rows))
    weight_total = lax.psum(weight_low, "leaf")
    def backward_part():
        output_gradient = contract_cols(shard_rows, out_weight).astype(jnp.bfloat16)
        key_acc = jnp.zeros((tree_len, kv_local, HEAD_SIZE), jnp.float32)
        value_acc = jnp.zeros((tree_len, kv_local, HEAD_SIZE), jnp.float32)
        query_parts = []
        for head_id in range(heads_local):
            kv_id = head_id // queries_per_group
            inner = head_id % queries_per_group
            query_blocks = []
            for block_id in range(block_total):
                opening_slot = block_id * block_len
                closing_slot = opening_slot + block_len
                query_now = asking_matrix[opening_slot:closing_slot, kv_id, inner]
                keys_now = lookup_matrix[:closing_slot, kv_id]
                values_now = value_rows[:closing_slot, kv_id]
                line_multiplier = softness_multiplier[opening_slot:closing_slot][:, None]
                attention_logits = jnp.where(
                    masks[block_id], contract_cols(query_now, keys_now) * line_multiplier, -jnp.inf
                )
                attention_probabilities = jnp.exp(
                    attention_logits - log_totals[kv_id, inner, opening_slot:closing_slot][:, None]
                )
                grad_rows = output_gradient[
                    opening_slot:closing_slot, head_id * HEAD_SIZE : (head_id + 1) * HEAD_SIZE
                ]
                own_rows = attended[opening_slot:closing_slot, kv_id, inner]
                probability_cotangent = contract_cols(grad_rows, values_now)
                middle_point = jnp.sum(
                    grad_rows.astype(jnp.float32) * own_rows.astype(jnp.float32), axis=1
                )
                logit_cotangent = (
                    attention_probabilities
                    * (probability_cotangent - middle_point[:, None])
                    * line_multiplier
                ).astype(jnp.bfloat16)
                query_blocks.append(
                    jnp.dot(logit_cotangent, keys_now, preferred_element_type=jnp.float32).astype(
                        jnp.bfloat16
                    )
                )
                key_acc = key_acc.at[:closing_slot, kv_id].add(
                    contract_rows(logit_cotangent, query_now)
                )
                value_acc = value_acc.at[:closing_slot, kv_id].add(
                    contract_rows(attention_probabilities.astype(jnp.bfloat16), grad_rows)
                )
            query_parts.append(jnp.concatenate(query_blocks, axis=0))
        query_grad = jnp.stack(query_parts, axis=1).reshape(
            tree_len, kv_local, queries_per_group, HEAD_SIZE
        )
        gradients = jnp.concatenate(
            [
                query_grad,
                key_acc.astype(jnp.bfloat16)[:, :, None],
                value_acc.astype(jnp.bfloat16)[:, :, None],
            ],
            axis=2,
        )
        gradients = gradients.reshape(tree_len, kv_local * (queries_per_group + 2) * HEAD_SIZE)
        return gradients

    def no_part():
        return jnp.zeros((tree_len, kv_local * (queries_per_group + 2) * HEAD_SIZE), jnp.bfloat16)

    gradients = lax.cond(lax.axis_index("ctx") >= 0, backward_part, no_part)
    returned = lax.all_to_all(gradients, "ctx", split_axis=0, concat_axis=1, tiled=True)
    return (returned, weight_total)


def solution(mesh):
    placed = (
        P(("leaf", "ctx"), None),
        P(("leaf", "ctx"), None),
        P("ctx", None),
        P("leaf", None),
        P("leaf"),
    )
    return jax.shard_map(
        local,
        mesh=mesh,
        in_specs=placed,
        out_specs=(P(("leaf", "ctx"), None), P("ctx", None)),
        check_vma=False,
    )
```

```python
import math

import jax
import jax.numpy as jnp
from jax import lax
from jax.sharding import PartitionSpec as P

QUERY_HEADS = 40
KEY_VALUE_HEADS = 8
HEAD_SIZE = 128
BLK = 128


log_base = 1024.0


def ancestors(parents):
    number = parents.shape[0]
    indices = jnp.arange(number, dtype=jnp.int32)

    def advance(iteration, state):
        current, reached = state
        current = jnp.sum(
            jnp.where(current[:, None] == indices[None, :], parents[None, :], 0), axis=1
        )
        return (current, reached | (current[:, None] == indices[None, :]))

    return lax.fori_loop(0, number, advance, (indices, indices[:, None] == indices[None, :]))[1]


def token_mask(reached, first_row, query_count, key_count):
    query_pos = first_row + jnp.arange(query_count, dtype=jnp.int32)
    key_pos = jnp.arange(key_count, dtype=jnp.int32)
    block_part = reached[first_row // BLK : (first_row + query_count) // BLK, : key_count // BLK]
    expanded = jnp.repeat(jnp.repeat(block_part, BLK, axis=0), BLK, axis=1)
    same_block = (query_pos // BLK)[:, None] == (key_pos // BLK)[None, :]
    return expanded & (jnp.logical_not(same_block) | (key_pos[None, :] <= query_pos[:, None]))


def span_softness(rollout_spans):
    return jnp.log(rollout_spans.astype(jnp.float32)) * (
        1.0 / (math.log(log_base) * math.sqrt(HEAD_SIZE))
    )


def contract_rows(left, right):
    return lax.dot_general(
        left, right, (((0,), (0,)), ((), ())), preferred_element_type=jnp.float32
    )


def contract_cols(left, right):
    return lax.dot_general(
        left, right, (((1,), (1,)), ((), ())), preferred_element_type=jnp.float32
    )


def local(query_key_value_rows, cotangent, out_weight, parents, rollout_spans):
    queries_per_group = QUERY_HEADS // KEY_VALUE_HEADS
    head_rows = lax.all_to_all(query_key_value_rows, "ctx", split_axis=1, concat_axis=0, tiled=True)
    tree_len = head_rows.shape[0]
    kv_local = head_rows.shape[1] // ((queries_per_group + 2) * HEAD_SIZE)
    heads_local = kv_local * queries_per_group
    grouped = head_rows.reshape(tree_len, kv_local, queries_per_group + 2, HEAD_SIZE)
    asking_matrix = grouped[:, :, :queries_per_group]
    lookup_matrix = grouped[:, :, queries_per_group]
    value_rows = grouped[:, :, queries_per_group + 1]
    softness_multiplier = span_softness(rollout_spans)
    reached = ancestors(parents[0])
    block_len = min(512, tree_len)
    block_total = tree_len // block_len
    masks = []
    total_parts = []
    attended_parts = []
    for block_id in range(block_total):
        opening_slot = block_id * block_len
        closing_slot = opening_slot + block_len
        allowed = token_mask(reached, opening_slot, block_len, closing_slot)
        masks.append(allowed)
        attention_logits = jnp.einsum(
            "zpyr,kpr->pyzk",
            asking_matrix[opening_slot:closing_slot],
            lookup_matrix[:closing_slot],
            preferred_element_type=jnp.float32,
        )
        attention_logits = jnp.where(
            allowed[None, None],
            attention_logits * softness_multiplier[opening_slot:closing_slot][None, None, :, None],
            -jnp.inf,
        )
        peak_score = jnp.max(attention_logits, axis=-1, keepdims=True)
        log_total = peak_score + jnp.log(
            jnp.sum(jnp.exp(attention_logits - peak_score), axis=-1, keepdims=True)
        )
        weights_low = jnp.exp(attention_logits - log_total).astype(jnp.bfloat16)
        attended_parts.append(
            jnp.einsum(
                "gjts,sgd->tgjd",
                weights_low,
                value_rows[:closing_slot],
                preferred_element_type=jnp.float32,
            ).astype(jnp.bfloat16)
        )
        total_parts.append(log_total[..., 0])
    attended = jnp.concatenate(attended_parts, axis=0)
    log_totals = jnp.concatenate(total_parts, axis=2)
    flat_out = attended.reshape(tree_len, heads_local * HEAD_SIZE)
    shard_rows = lax.all_gather(cotangent, "ctx", axis=0, tiled=True)
    weight_low = contract_rows(flat_out, shard_rows).astype(jnp.bfloat16)
    weight_low, shard_rows = lax.optimization_barrier((weight_low, shard_rows))
    weight_total = lax.psum(weight_low, "leaf")
    def backward_part():
        output_gradient = contract_cols(shard_rows, out_weight).astype(jnp.bfloat16)
        asking_heads = jnp.transpose(asking_matrix.reshape(tree_len, heads_local, HEAD_SIZE), (1, 0, 2))
        attended_heads = jnp.transpose(attended.reshape(tree_len, heads_local, HEAD_SIZE), (1, 0, 2))
        grad_heads = jnp.transpose(output_gradient.reshape(tree_len, heads_local, HEAD_SIZE), (1, 0, 2))
        totals_heads = log_totals.reshape(heads_local, tree_len)

        def one_head(head_id, carry):
            key_acc, value_acc, query_grad = carry
            kv_id = head_id // queries_per_group
            keys_all = lax.dynamic_index_in_dim(lookup_matrix, kv_id, axis=1, keepdims=False)
            values_all = lax.dynamic_index_in_dim(value_rows, kv_id, axis=1, keepdims=False)
            query_all = lax.dynamic_index_in_dim(asking_heads, head_id, axis=0, keepdims=False)
            grad_all = lax.dynamic_index_in_dim(grad_heads, head_id, axis=0, keepdims=False)
            own_all = lax.dynamic_index_in_dim(attended_heads, head_id, axis=0, keepdims=False)
            totals_all = lax.dynamic_index_in_dim(totals_heads, head_id, axis=0, keepdims=False)
            key_now = lax.dynamic_index_in_dim(key_acc, kv_id, axis=1, keepdims=False)
            value_now = lax.dynamic_index_in_dim(value_acc, kv_id, axis=1, keepdims=False)
            query_blocks = []
            for block_id in range(block_total):
                opening_slot = block_id * block_len
                closing_slot = opening_slot + block_len
                query_now = query_all[opening_slot:closing_slot]
                keys_now = keys_all[:closing_slot]
                values_now = values_all[:closing_slot]
                line_multiplier = softness_multiplier[opening_slot:closing_slot][:, None]
                attention_logits = jnp.where(
                    masks[block_id], contract_cols(query_now, keys_now) * line_multiplier, -jnp.inf
                )
                attention_probabilities = jnp.exp(
                    attention_logits - totals_all[opening_slot:closing_slot][:, None]
                )
                grad_rows = grad_all[opening_slot:closing_slot]
                own_rows = own_all[opening_slot:closing_slot]
                probability_cotangent = contract_cols(grad_rows, values_now)
                middle_point = jnp.sum(
                    grad_rows.astype(jnp.float32) * own_rows.astype(jnp.float32), axis=1
                )
                logit_cotangent = (
                    attention_probabilities
                    * (probability_cotangent - middle_point[:, None])
                    * line_multiplier
                ).astype(jnp.bfloat16)
                query_blocks.append(
                    jnp.dot(logit_cotangent, keys_now, preferred_element_type=jnp.float32).astype(
                        jnp.bfloat16
                    )
                )
                key_now = key_now.at[:closing_slot].add(contract_rows(logit_cotangent, query_now))
                value_now = value_now.at[:closing_slot].add(
                    contract_rows(attention_probabilities.astype(jnp.bfloat16), grad_rows)
                )
            key_acc = lax.dynamic_update_index_in_dim(key_acc, key_now, kv_id, axis=1)
            value_acc = lax.dynamic_update_index_in_dim(value_acc, value_now, kv_id, axis=1)
            query_grad = lax.dynamic_update_index_in_dim(
                query_grad, jnp.concatenate(query_blocks, axis=0), head_id, axis=0
            )
            return key_acc, value_acc, query_grad

        key_acc, value_acc, query_grad = lax.fori_loop(
            0,
            heads_local,
            one_head,
            (
                jnp.zeros((tree_len, kv_local, HEAD_SIZE), jnp.float32),
                jnp.zeros((tree_len, kv_local, HEAD_SIZE), jnp.float32),
                jnp.zeros((heads_local, tree_len, HEAD_SIZE), jnp.bfloat16),
            ),
        )
        query_grad = jnp.transpose(query_grad, (1, 0, 2)).reshape(
            tree_len, kv_local, queries_per_group, HEAD_SIZE
        )
        gradients = jnp.concatenate(
            [
                query_grad,
                key_acc.astype(jnp.bfloat16)[:, :, None],
                value_acc.astype(jnp.bfloat16)[:, :, None],
            ],
            axis=2,
        )
        gradients = gradients.reshape(tree_len, kv_local * (queries_per_group + 2) * HEAD_SIZE)
        return gradients

    def no_part():
        return jnp.zeros((tree_len, kv_local * (queries_per_group + 2) * HEAD_SIZE), jnp.bfloat16)

    gradients = lax.cond(lax.axis_index("ctx") >= 0, backward_part, no_part)
    returned = lax.all_to_all(gradients, "ctx", split_axis=0, concat_axis=1, tiled=True)
    return (returned, weight_total)


def solution(mesh):
    placed = (
        P(("leaf", "ctx"), None),
        P(("leaf", "ctx"), None),
        P("ctx", None),
        P("leaf", None),
        P("leaf"),
    )
    return jax.shard_map(
        local,
        mesh=mesh,
        in_specs=placed,
        out_specs=(P(("leaf", "ctx"), None), P("ctx", None)),
        check_vma=False,
    )
```

```python
import math

import jax
import jax.numpy as jnp
from jax import lax
from jax.sharding import PartitionSpec as P

QUERY_HEADS = 40
KEY_VALUE_HEADS = 8
HEAD_SIZE = 128
BLK = 128


log_base = 1024.0


def ancestors(parents):
    number = parents.shape[0]
    indices = jnp.arange(number, dtype=jnp.int32)

    def advance(iteration, state):
        current, reached = state
        current = jnp.sum(
            jnp.where(current[:, None] == indices[None, :], parents[None, :], 0), axis=1
        )
        return (current, reached | (current[:, None] == indices[None, :]))

    return lax.fori_loop(0, number, advance, (indices, indices[:, None] == indices[None, :]))[1]


def token_mask(reached, first_row, query_count, key_count):
    query_pos = first_row + jnp.arange(query_count, dtype=jnp.int32)
    key_pos = jnp.arange(key_count, dtype=jnp.int32)
    block_part = reached[first_row // BLK : (first_row + query_count) // BLK, : key_count // BLK]
    expanded = jnp.repeat(jnp.repeat(block_part, BLK, axis=0), BLK, axis=1)
    same_block = (query_pos // BLK)[:, None] == (key_pos // BLK)[None, :]
    return expanded & (jnp.logical_not(same_block) | (key_pos[None, :] <= query_pos[:, None]))


def span_softness(rollout_spans):
    return jnp.log(rollout_spans.astype(jnp.float32)) * (
        1.0 / (math.log(log_base) * math.sqrt(HEAD_SIZE))
    )


def contract_rows(left, right):
    return lax.dot_general(
        left, right, (((0,), (0,)), ((), ())), preferred_element_type=jnp.float32
    )


def contract_cols(left, right):
    return lax.dot_general(
        left, right, (((1,), (1,)), ((), ())), preferred_element_type=jnp.float32
    )


def local(query_key_value_rows, cotangent, out_weight, parents, rollout_spans):
    queries_per_group = QUERY_HEADS // KEY_VALUE_HEADS
    head_rows = lax.all_to_all(query_key_value_rows, "ctx", split_axis=1, concat_axis=0, tiled=True)
    tree_len = head_rows.shape[0]
    kv_local = head_rows.shape[1] // ((queries_per_group + 2) * HEAD_SIZE)
    heads_local = kv_local * queries_per_group
    grouped = head_rows.reshape(tree_len, kv_local, queries_per_group + 2, HEAD_SIZE)
    asking_matrix = grouped[:, :, :queries_per_group]
    lookup_matrix = grouped[:, :, queries_per_group]
    value_rows = grouped[:, :, queries_per_group + 1]
    softness_multiplier = span_softness(rollout_spans)
    reached = ancestors(parents[0])
    block_len = min(512, tree_len)
    block_total = tree_len // block_len
    masks = []
    total_parts = []
    attended_parts = []
    for block_id in range(block_total):
        opening_slot = block_id * block_len
        closing_slot = opening_slot + block_len
        allowed = token_mask(reached, opening_slot, block_len, closing_slot)
        masks.append(allowed)
        attention_logits = jnp.einsum(
            "zpyr,kpr->pyzk",
            asking_matrix[opening_slot:closing_slot],
            lookup_matrix[:closing_slot],
            preferred_element_type=jnp.float32,
        )
        attention_logits = jnp.where(
            allowed[None, None],
            attention_logits * softness_multiplier[opening_slot:closing_slot][None, None, :, None],
            -jnp.inf,
        )
        peak_score = jnp.max(attention_logits, axis=-1, keepdims=True)
        log_total = peak_score + jnp.log(
            jnp.sum(jnp.exp(attention_logits - peak_score), axis=-1, keepdims=True)
        )
        weights_low = jnp.exp(attention_logits - log_total).astype(jnp.bfloat16)
        attended_parts.append(
            jnp.einsum(
                "gjts,sgd->tgjd",
                weights_low,
                value_rows[:closing_slot],
                preferred_element_type=jnp.float32,
            ).astype(jnp.bfloat16)
        )
        total_parts.append(log_total[..., 0])
    attended = jnp.concatenate(attended_parts, axis=0)
    log_totals = jnp.concatenate(total_parts, axis=2)
    flat_out = attended.reshape(tree_len, heads_local * HEAD_SIZE)
    shard_rows = lax.all_gather(cotangent, "ctx", axis=0, tiled=True)
    weight_low = contract_rows(flat_out, shard_rows).astype(jnp.bfloat16)
    weight_low, shard_rows = lax.optimization_barrier((weight_low, shard_rows))
    weight_total = lax.psum(weight_low, "leaf")
    def backward_part():
        output_gradient = contract_cols(shard_rows, out_weight).astype(jnp.bfloat16)
        asking_heads = jnp.transpose(asking_matrix.reshape(tree_len, heads_local, HEAD_SIZE), (1, 0, 2))
        attended_heads = jnp.transpose(attended.reshape(tree_len, heads_local, HEAD_SIZE), (1, 0, 2))
        grad_heads = jnp.transpose(output_gradient.reshape(tree_len, heads_local, HEAD_SIZE), (1, 0, 2))
        totals_heads = log_totals.reshape(heads_local, tree_len)

        def one_head(head_id, carry):
            key_acc, value_acc, query_grad = carry
            kv_id = head_id // queries_per_group
            keys_all = lax.dynamic_index_in_dim(lookup_matrix, kv_id, axis=1, keepdims=False)
            values_all = lax.dynamic_index_in_dim(value_rows, kv_id, axis=1, keepdims=False)
            query_all = lax.dynamic_index_in_dim(asking_heads, head_id, axis=0, keepdims=False)
            grad_all = lax.dynamic_index_in_dim(grad_heads, head_id, axis=0, keepdims=False)
            own_all = lax.dynamic_index_in_dim(attended_heads, head_id, axis=0, keepdims=False)
            totals_all = lax.dynamic_index_in_dim(totals_heads, head_id, axis=0, keepdims=False)
            key_now = lax.dynamic_index_in_dim(key_acc, kv_id, axis=1, keepdims=False)
            value_now = lax.dynamic_index_in_dim(value_acc, kv_id, axis=1, keepdims=False)
            query_blocks = []
            for block_id in range(block_total):
                opening_slot = block_id * block_len
                closing_slot = opening_slot + block_len
                query_now = query_all[opening_slot:closing_slot]
                keys_now = keys_all[:closing_slot]
                values_now = values_all[:closing_slot]
                line_multiplier = softness_multiplier[opening_slot:closing_slot][:, None]
                allowed_now = token_mask(reached, opening_slot, block_len, closing_slot)
                attention_logits = jnp.where(
                    allowed_now, contract_cols(query_now, keys_now) * line_multiplier, -jnp.inf
                )
                attention_probabilities = jnp.exp(
                    attention_logits - totals_all[opening_slot:closing_slot][:, None]
                )
                grad_rows = grad_all[opening_slot:closing_slot]
                own_rows = own_all[opening_slot:closing_slot]
                probability_cotangent = contract_cols(grad_rows, values_now)
                middle_point = jnp.sum(
                    grad_rows.astype(jnp.float32) * own_rows.astype(jnp.float32), axis=1
                )
                logit_cotangent = (
                    attention_probabilities
                    * (probability_cotangent - middle_point[:, None])
                    * line_multiplier
                ).astype(jnp.bfloat16)
                query_blocks.append(
                    jnp.dot(logit_cotangent, keys_now, preferred_element_type=jnp.float32).astype(
                        jnp.bfloat16
                    )
                )
                key_now = key_now.at[:closing_slot].add(contract_rows(logit_cotangent, query_now))
                value_now = value_now.at[:closing_slot].add(
                    contract_rows(attention_probabilities.astype(jnp.bfloat16), grad_rows)
                )
            key_acc = lax.dynamic_update_index_in_dim(key_acc, key_now, kv_id, axis=1)
            value_acc = lax.dynamic_update_index_in_dim(value_acc, value_now, kv_id, axis=1)
            query_grad = lax.dynamic_update_index_in_dim(
                query_grad, jnp.concatenate(query_blocks, axis=0), head_id, axis=0
            )
            return key_acc, value_acc, query_grad

        key_acc, value_acc, query_grad = lax.fori_loop(
            0,
            heads_local,
            one_head,
            (
                jnp.zeros((tree_len, kv_local, HEAD_SIZE), jnp.float32),
                jnp.zeros((tree_len, kv_local, HEAD_SIZE), jnp.float32),
                jnp.zeros((heads_local, tree_len, HEAD_SIZE), jnp.bfloat16),
            ),
        )
        query_grad = jnp.transpose(query_grad, (1, 0, 2)).reshape(
            tree_len, kv_local, queries_per_group, HEAD_SIZE
        )
        gradients = jnp.concatenate(
            [
                query_grad,
                key_acc.astype(jnp.bfloat16)[:, :, None],
                value_acc.astype(jnp.bfloat16)[:, :, None],
            ],
            axis=2,
        )
        gradients = gradients.reshape(tree_len, kv_local * (queries_per_group + 2) * HEAD_SIZE)
        return gradients

    def no_part():
        return jnp.zeros((tree_len, kv_local * (queries_per_group + 2) * HEAD_SIZE), jnp.bfloat16)

    gradients = lax.cond(lax.axis_index("ctx") >= 0, backward_part, no_part)
    returned = lax.all_to_all(gradients, "ctx", split_axis=0, concat_axis=1, tiled=True)
    return (returned, weight_total)


def solution(mesh):
    placed = (
        P(("leaf", "ctx"), None),
        P(("leaf", "ctx"), None),
        P("ctx", None),
        P("leaf", None),
        P("leaf"),
    )
    return jax.shard_map(
        local,
        mesh=mesh,
        in_specs=placed,
        out_specs=(P(("leaf", "ctx"), None), P("ctx", None)),
        check_vma=False,
    )
```

```python
import math

import jax
import jax.numpy as jnp
from jax import lax
from jax.sharding import PartitionSpec as P

QUERY_HEADS = 40
KEY_VALUE_HEADS = 8
HEAD_SIZE = 128
BLK = 128


log_base = 1024.0


def ancestors(parents):
    number = parents.shape[0]
    indices = jnp.arange(number, dtype=jnp.int32)

    def advance(iteration, state):
        current, reached = state
        current = jnp.sum(
            jnp.where(current[:, None] == indices[None, :], parents[None, :], 0), axis=1
        )
        return (current, reached | (current[:, None] == indices[None, :]))

    return lax.fori_loop(0, number, advance, (indices, indices[:, None] == indices[None, :]))[1]


def token_mask(reached, first_row, query_count, key_count):
    query_pos = first_row + jnp.arange(query_count, dtype=jnp.int32)
    key_pos = jnp.arange(key_count, dtype=jnp.int32)
    block_part = reached[first_row // BLK : (first_row + query_count) // BLK, : key_count // BLK]
    expanded = jnp.repeat(jnp.repeat(block_part, BLK, axis=0), BLK, axis=1)
    same_block = (query_pos // BLK)[:, None] == (key_pos // BLK)[None, :]
    return expanded & (jnp.logical_not(same_block) | (key_pos[None, :] <= query_pos[:, None]))


def span_softness(rollout_spans):
    return jnp.log(rollout_spans.astype(jnp.float32)) * (
        1.0 / (math.log(log_base) * math.sqrt(HEAD_SIZE))
    )


def contract_rows(left, right):
    return lax.dot_general(
        left, right, (((0,), (0,)), ((), ())), preferred_element_type=jnp.float32
    )


def contract_cols(left, right):
    return lax.dot_general(
        left, right, (((1,), (1,)), ((), ())), preferred_element_type=jnp.float32
    )


def local(query_key_value_rows, cotangent, out_weight, parents, rollout_spans):
    queries_per_group = QUERY_HEADS // KEY_VALUE_HEADS
    head_rows = lax.all_to_all(query_key_value_rows, "ctx", split_axis=1, concat_axis=0, tiled=True)
    tree_len = head_rows.shape[0]
    kv_local = head_rows.shape[1] // ((queries_per_group + 2) * HEAD_SIZE)
    heads_local = kv_local * queries_per_group
    grouped = head_rows.reshape(tree_len, kv_local, queries_per_group + 2, HEAD_SIZE)
    asking_matrix = grouped[:, :, :queries_per_group]
    lookup_matrix = grouped[:, :, queries_per_group]
    value_rows = grouped[:, :, queries_per_group + 1]
    softness_multiplier = span_softness(rollout_spans)
    reached = ancestors(parents[0])
    block_len = min(512, tree_len)
    block_total = tree_len // block_len
    masks = []
    total_parts = []
    attended_parts = []
    for block_id in range(block_total):
        opening_slot = block_id * block_len
        closing_slot = opening_slot + block_len
        allowed = token_mask(reached, opening_slot, block_len, closing_slot)
        masks.append(allowed)
        attention_logits = jnp.einsum(
            "zpyr,kpr->pyzk",
            asking_matrix[opening_slot:closing_slot],
            lookup_matrix[:closing_slot],
            preferred_element_type=jnp.float32,
        )
        attention_logits = jnp.where(
            allowed[None, None],
            attention_logits * softness_multiplier[opening_slot:closing_slot][None, None, :, None],
            -jnp.inf,
        )
        peak_score = jnp.max(attention_logits, axis=-1, keepdims=True)
        log_total = peak_score + jnp.log(
            jnp.sum(jnp.exp(attention_logits - peak_score), axis=-1, keepdims=True)
        )
        weights_low = jnp.exp(attention_logits - log_total).astype(jnp.bfloat16)
        attended_parts.append(
            jnp.einsum(
                "gjts,sgd->tgjd",
                weights_low,
                value_rows[:closing_slot],
                preferred_element_type=jnp.float32,
            ).astype(jnp.bfloat16)
        )
        total_parts.append(log_total[..., 0])
    attended = jnp.concatenate(attended_parts, axis=0)
    log_totals = jnp.concatenate(total_parts, axis=2)
    flat_out = attended.reshape(tree_len, heads_local * HEAD_SIZE)
    shard_rows = lax.all_gather(cotangent, "ctx", axis=0, tiled=True)
    weight_low = contract_rows(flat_out, shard_rows).astype(jnp.bfloat16)
    weight_low, shard_rows, masks = lax.optimization_barrier((weight_low, shard_rows, masks))
    weight_total = lax.psum(weight_low, "leaf")
    def backward_part():
        output_gradient = contract_cols(shard_rows, out_weight).astype(jnp.bfloat16)
        asking_heads = jnp.transpose(asking_matrix.reshape(tree_len, heads_local, HEAD_SIZE), (1, 0, 2))
        attended_heads = jnp.transpose(attended.reshape(tree_len, heads_local, HEAD_SIZE), (1, 0, 2))
        grad_heads = jnp.transpose(output_gradient.reshape(tree_len, heads_local, HEAD_SIZE), (1, 0, 2))
        totals_heads = log_totals.reshape(heads_local, tree_len)

        def one_head(head_id, carry):
            key_acc, value_acc, query_grad = carry
            kv_id = head_id // queries_per_group
            keys_all = lax.dynamic_index_in_dim(lookup_matrix, kv_id, axis=1, keepdims=False)
            values_all = lax.dynamic_index_in_dim(value_rows, kv_id, axis=1, keepdims=False)
            query_all = lax.dynamic_index_in_dim(asking_heads, head_id, axis=0, keepdims=False)
            grad_all = lax.dynamic_index_in_dim(grad_heads, head_id, axis=0, keepdims=False)
            own_all = lax.dynamic_index_in_dim(attended_heads, head_id, axis=0, keepdims=False)
            totals_all = lax.dynamic_index_in_dim(totals_heads, head_id, axis=0, keepdims=False)
            key_now = lax.dynamic_index_in_dim(key_acc, kv_id, axis=1, keepdims=False)
            value_now = lax.dynamic_index_in_dim(value_acc, kv_id, axis=1, keepdims=False)
            query_blocks = []
            for block_id in range(block_total):
                opening_slot = block_id * block_len
                closing_slot = opening_slot + block_len
                query_now = query_all[opening_slot:closing_slot]
                keys_now = keys_all[:closing_slot]
                values_now = values_all[:closing_slot]
                line_multiplier = softness_multiplier[opening_slot:closing_slot][:, None]
                attention_logits = jnp.where(
                    masks[block_id], contract_cols(query_now, keys_now) * line_multiplier, -jnp.inf
                )
                attention_probabilities = jnp.exp(
                    attention_logits - totals_all[opening_slot:closing_slot][:, None]
                )
                grad_rows = grad_all[opening_slot:closing_slot]
                own_rows = own_all[opening_slot:closing_slot]
                probability_cotangent = contract_cols(grad_rows, values_now)
                middle_point = jnp.sum(
                    grad_rows.astype(jnp.float32) * own_rows.astype(jnp.float32), axis=1
                )
                logit_cotangent = (
                    attention_probabilities
                    * (probability_cotangent - middle_point[:, None])
                    * line_multiplier
                ).astype(jnp.bfloat16)
                query_blocks.append(
                    jnp.dot(logit_cotangent, keys_now, preferred_element_type=jnp.float32).astype(
                        jnp.bfloat16
                    )
                )
                key_now = key_now.at[:closing_slot].add(contract_rows(logit_cotangent, query_now))
                value_now = value_now.at[:closing_slot].add(
                    contract_rows(attention_probabilities.astype(jnp.bfloat16), grad_rows)
                )
            key_acc = lax.dynamic_update_index_in_dim(key_acc, key_now, kv_id, axis=1)
            value_acc = lax.dynamic_update_index_in_dim(value_acc, value_now, kv_id, axis=1)
            query_grad = lax.dynamic_update_index_in_dim(
                query_grad, jnp.concatenate(query_blocks, axis=0), head_id, axis=0
            )
            return key_acc, value_acc, query_grad

        key_acc, value_acc, query_grad = lax.fori_loop(
            0,
            heads_local,
            one_head,
            (
                jnp.zeros((tree_len, kv_local, HEAD_SIZE), jnp.float32),
                jnp.zeros((tree_len, kv_local, HEAD_SIZE), jnp.float32),
                jnp.zeros((heads_local, tree_len, HEAD_SIZE), jnp.bfloat16),
            ),
        )
        query_grad = jnp.transpose(query_grad, (1, 0, 2)).reshape(
            tree_len, kv_local, queries_per_group, HEAD_SIZE
        )
        gradients = jnp.concatenate(
            [
                query_grad,
                key_acc.astype(jnp.bfloat16)[:, :, None],
                value_acc.astype(jnp.bfloat16)[:, :, None],
            ],
            axis=2,
        )
        gradients = gradients.reshape(tree_len, kv_local * (queries_per_group + 2) * HEAD_SIZE)
        return gradients

    def no_part():
        return jnp.zeros((tree_len, kv_local * (queries_per_group + 2) * HEAD_SIZE), jnp.bfloat16)

    gradients = lax.cond(lax.axis_index("ctx") >= 0, backward_part, no_part)
    returned = lax.all_to_all(gradients, "ctx", split_axis=0, concat_axis=1, tiled=True)
    return (returned, weight_total)


def solution(mesh):
    placed = (
        P(("leaf", "ctx"), None),
        P(("leaf", "ctx"), None),
        P("ctx", None),
        P("leaf", None),
        P("leaf"),
    )
    return jax.shard_map(
        local,
        mesh=mesh,
        in_specs=placed,
        out_specs=(P(("leaf", "ctx"), None), P("ctx", None)),
        check_vma=False,
    )
```

```python
import math

import jax
import jax.numpy as jnp
from jax import lax
from jax.sharding import PartitionSpec as P

QUERY_HEADS = 40
KEY_VALUE_HEADS = 8
HEAD_SIZE = 128
BLK = 128


log_base = 1024.0


def ancestors(parents):
    number = parents.shape[0]
    indices = jnp.arange(number, dtype=jnp.int32)

    def advance(iteration, state):
        current, reached = state
        current = jnp.sum(
            jnp.where(current[:, None] == indices[None, :], parents[None, :], 0), axis=1
        )
        return (current, reached | (current[:, None] == indices[None, :]))

    return lax.fori_loop(0, number, advance, (indices, indices[:, None] == indices[None, :]))[1]


def token_mask(reached, first_row, query_count, key_count):
    query_pos = first_row + jnp.arange(query_count, dtype=jnp.int32)
    key_pos = jnp.arange(key_count, dtype=jnp.int32)
    block_part = reached[first_row // BLK : (first_row + query_count) // BLK, : key_count // BLK]
    expanded = jnp.repeat(jnp.repeat(block_part, BLK, axis=0), BLK, axis=1)
    same_block = (query_pos // BLK)[:, None] == (key_pos // BLK)[None, :]
    return expanded & (jnp.logical_not(same_block) | (key_pos[None, :] <= query_pos[:, None]))


def span_softness(rollout_spans):
    return jnp.log(rollout_spans.astype(jnp.float32)) * (
        1.0 / (math.log(log_base) * math.sqrt(HEAD_SIZE))
    )


def contract_rows(left, right):
    return lax.dot_general(
        left, right, (((0,), (0,)), ((), ())), preferred_element_type=jnp.float32
    )


def contract_cols(left, right):
    return lax.dot_general(
        left, right, (((1,), (1,)), ((), ())), preferred_element_type=jnp.float32
    )


def local(query_key_value_rows, cotangent, out_weight, parents, rollout_spans):
    queries_per_group = QUERY_HEADS // KEY_VALUE_HEADS
    head_rows = lax.all_to_all(query_key_value_rows, "ctx", split_axis=1, concat_axis=0, tiled=True)
    tree_len = head_rows.shape[0]
    kv_local = head_rows.shape[1] // ((queries_per_group + 2) * HEAD_SIZE)
    heads_local = kv_local * queries_per_group
    grouped = head_rows.reshape(tree_len, kv_local, queries_per_group + 2, HEAD_SIZE)
    asking_matrix = grouped[:, :, :queries_per_group]
    lookup_matrix = grouped[:, :, queries_per_group]
    value_rows = grouped[:, :, queries_per_group + 1]
    softness_multiplier = span_softness(rollout_spans)
    reached = ancestors(parents[0])
    block_len = min(512, tree_len)
    block_total = tree_len // block_len
    masks = []
    total_parts = []
    attended_parts = []
    for block_id in range(block_total):
        opening_slot = block_id * block_len
        closing_slot = opening_slot + block_len
        allowed = token_mask(reached, opening_slot, block_len, closing_slot)
        masks.append(allowed)
        attention_logits = jnp.einsum(
            "zpyr,kpr->pyzk",
            asking_matrix[opening_slot:closing_slot],
            lookup_matrix[:closing_slot],
            preferred_element_type=jnp.float32,
        )
        attention_logits = jnp.where(
            allowed[None, None],
            attention_logits * softness_multiplier[opening_slot:closing_slot][None, None, :, None],
            -jnp.inf,
        )
        peak_score = jnp.max(attention_logits, axis=-1, keepdims=True)
        log_total = peak_score + jnp.log(
            jnp.sum(jnp.exp(attention_logits - peak_score), axis=-1, keepdims=True)
        )
        weights_low = jnp.exp(attention_logits - log_total).astype(jnp.bfloat16)
        attended_parts.append(
            jnp.einsum(
                "gjts,sgd->tgjd",
                weights_low,
                value_rows[:closing_slot],
                preferred_element_type=jnp.float32,
            ).astype(jnp.bfloat16)
        )
        total_parts.append(log_total[..., 0])
    attended = jnp.concatenate(attended_parts, axis=0)
    log_totals = jnp.concatenate(total_parts, axis=2)
    flat_out = attended.reshape(tree_len, heads_local * HEAD_SIZE)
    shard_rows = lax.all_gather(cotangent, "ctx", axis=0, tiled=True)
    weight_low = contract_rows(flat_out, shard_rows).astype(jnp.bfloat16)
    asking_heads = jnp.transpose(asking_matrix.reshape(tree_len, heads_local, HEAD_SIZE), (1, 0, 2))
    attended_heads = jnp.transpose(attended.reshape(tree_len, heads_local, HEAD_SIZE), (1, 0, 2))
    (
        weight_low, shard_rows, masks, asking_heads, attended_heads, lookup_matrix, value_rows, log_totals
    ) = lax.optimization_barrier(
        (weight_low, shard_rows, masks, asking_heads, attended_heads, lookup_matrix, value_rows, log_totals)
    )
    weight_total = lax.psum(weight_low, "leaf")
    def backward_part():
        output_gradient = contract_cols(shard_rows, out_weight).astype(jnp.bfloat16)
        grad_heads = jnp.transpose(output_gradient.reshape(tree_len, heads_local, HEAD_SIZE), (1, 0, 2))
        totals_heads = log_totals.reshape(heads_local, tree_len)

        def one_head(head_id, carry):
            key_acc, value_acc, query_grad = carry
            kv_id = head_id // queries_per_group
            keys_all = lax.dynamic_index_in_dim(lookup_matrix, kv_id, axis=1, keepdims=False)
            values_all = lax.dynamic_index_in_dim(value_rows, kv_id, axis=1, keepdims=False)
            query_all = lax.dynamic_index_in_dim(asking_heads, head_id, axis=0, keepdims=False)
            grad_all = lax.dynamic_index_in_dim(grad_heads, head_id, axis=0, keepdims=False)
            own_all = lax.dynamic_index_in_dim(attended_heads, head_id, axis=0, keepdims=False)
            totals_all = lax.dynamic_index_in_dim(totals_heads, head_id, axis=0, keepdims=False)
            key_now = lax.dynamic_index_in_dim(key_acc, kv_id, axis=1, keepdims=False)
            value_now = lax.dynamic_index_in_dim(value_acc, kv_id, axis=1, keepdims=False)
            query_blocks = []
            for block_id in range(block_total):
                opening_slot = block_id * block_len
                closing_slot = opening_slot + block_len
                query_now = query_all[opening_slot:closing_slot]
                keys_now = keys_all[:closing_slot]
                values_now = values_all[:closing_slot]
                line_multiplier = softness_multiplier[opening_slot:closing_slot][:, None]
                attention_logits = jnp.where(
                    masks[block_id], contract_cols(query_now, keys_now) * line_multiplier, -jnp.inf
                )
                attention_probabilities = jnp.exp(
                    attention_logits - totals_all[opening_slot:closing_slot][:, None]
                )
                grad_rows = grad_all[opening_slot:closing_slot]
                own_rows = own_all[opening_slot:closing_slot]
                probability_cotangent = contract_cols(grad_rows, values_now)
                middle_point = jnp.sum(
                    grad_rows.astype(jnp.float32) * own_rows.astype(jnp.float32), axis=1
                )
                logit_cotangent = (
                    attention_probabilities
                    * (probability_cotangent - middle_point[:, None])
                    * line_multiplier
                ).astype(jnp.bfloat16)
                query_blocks.append(
                    jnp.dot(logit_cotangent, keys_now, preferred_element_type=jnp.float32).astype(
                        jnp.bfloat16
                    )
                )
                key_now = key_now.at[:closing_slot].add(contract_rows(logit_cotangent, query_now))
                value_now = value_now.at[:closing_slot].add(
                    contract_rows(attention_probabilities.astype(jnp.bfloat16), grad_rows)
                )
            key_acc = lax.dynamic_update_index_in_dim(key_acc, key_now, kv_id, axis=1)
            value_acc = lax.dynamic_update_index_in_dim(value_acc, value_now, kv_id, axis=1)
            query_grad = lax.dynamic_update_index_in_dim(
                query_grad, jnp.concatenate(query_blocks, axis=0), head_id, axis=0
            )
            return key_acc, value_acc, query_grad

        key_acc, value_acc, query_grad = lax.fori_loop(
            0,
            heads_local,
            one_head,
            (
                jnp.zeros((tree_len, kv_local, HEAD_SIZE), jnp.float32),
                jnp.zeros((tree_len, kv_local, HEAD_SIZE), jnp.float32),
                jnp.zeros((heads_local, tree_len, HEAD_SIZE), jnp.bfloat16),
            ),
        )
        query_grad = jnp.transpose(query_grad, (1, 0, 2)).reshape(
            tree_len, kv_local, queries_per_group, HEAD_SIZE
        )
        gradients = jnp.concatenate(
            [
                query_grad,
                key_acc.astype(jnp.bfloat16)[:, :, None],
                value_acc.astype(jnp.bfloat16)[:, :, None],
            ],
            axis=2,
        )
        gradients = gradients.reshape(tree_len, kv_local * (queries_per_group + 2) * HEAD_SIZE)
        return gradients

    def no_part():
        return jnp.zeros((tree_len, kv_local * (queries_per_group + 2) * HEAD_SIZE), jnp.bfloat16)

    gradients = lax.cond(lax.axis_index("ctx") >= 0, backward_part, no_part)
    returned = lax.all_to_all(gradients, "ctx", split_axis=0, concat_axis=1, tiled=True)
    return (returned, weight_total)


def solution(mesh):
    placed = (
        P(("leaf", "ctx"), None),
        P(("leaf", "ctx"), None),
        P("ctx", None),
        P("leaf", None),
        P("leaf"),
    )
    return jax.shard_map(
        local,
        mesh=mesh,
        in_specs=placed,
        out_specs=(P(("leaf", "ctx"), None), P("ctx", None)),
        check_vma=False,
    )
```

```python
import math

import jax
import jax.numpy as jnp
from jax import lax
from jax.sharding import PartitionSpec as P

QUERY_HEADS = 40
KEY_VALUE_HEADS = 8
HEAD_SIZE = 128
BLK = 128


log_base = 1024.0


def ancestors(parents):
    number = parents.shape[0]
    indices = jnp.arange(number, dtype=jnp.int32)

    def advance(iteration, state):
        current, reached = state
        current = jnp.sum(
            jnp.where(current[:, None] == indices[None, :], parents[None, :], 0), axis=1
        )
        return (current, reached | (current[:, None] == indices[None, :]))

    return lax.fori_loop(0, number, advance, (indices, indices[:, None] == indices[None, :]))[1]


def token_mask(reached, first_row, query_count, key_count):
    query_pos = first_row + jnp.arange(query_count, dtype=jnp.int32)
    key_pos = jnp.arange(key_count, dtype=jnp.int32)
    block_part = reached[first_row // BLK : (first_row + query_count) // BLK, : key_count // BLK]
    expanded = jnp.repeat(jnp.repeat(block_part, BLK, axis=0), BLK, axis=1)
    same_block = (query_pos // BLK)[:, None] == (key_pos // BLK)[None, :]
    return expanded & (jnp.logical_not(same_block) | (key_pos[None, :] <= query_pos[:, None]))


def span_softness(rollout_spans):
    return jnp.log(rollout_spans.astype(jnp.float32)) * (
        1.0 / (math.log(log_base) * math.sqrt(HEAD_SIZE))
    )


def contract_rows(left, right):
    return lax.dot_general(
        left, right, (((0,), (0,)), ((), ())), preferred_element_type=jnp.float32
    )


def contract_cols(left, right):
    return lax.dot_general(
        left, right, (((1,), (1,)), ((), ())), preferred_element_type=jnp.float32
    )


def local(query_key_value_rows, cotangent, out_weight, parents, rollout_spans):
    queries_per_group = QUERY_HEADS // KEY_VALUE_HEADS
    head_rows = lax.all_to_all(query_key_value_rows, "ctx", split_axis=1, concat_axis=0, tiled=True)
    cotangent, head_rows = lax.optimization_barrier((cotangent, head_rows))
    tree_len = head_rows.shape[0]
    kv_local = head_rows.shape[1] // ((queries_per_group + 2) * HEAD_SIZE)
    heads_local = kv_local * queries_per_group
    grouped = head_rows.reshape(tree_len, kv_local, queries_per_group + 2, HEAD_SIZE)
    asking_matrix = grouped[:, :, :queries_per_group]
    lookup_matrix = grouped[:, :, queries_per_group]
    value_rows = grouped[:, :, queries_per_group + 1]
    softness_multiplier = span_softness(rollout_spans)
    reached = ancestors(parents[0])
    block_len = min(512, tree_len)
    block_total = tree_len // block_len
    masks = []
    total_parts = []
    attended_parts = []
    for block_id in range(block_total):
        opening_slot = block_id * block_len
        closing_slot = opening_slot + block_len
        allowed = token_mask(reached, opening_slot, block_len, closing_slot)
        masks.append(allowed)
        attention_logits = jnp.einsum(
            "zpyr,kpr->pyzk",
            asking_matrix[opening_slot:closing_slot],
            lookup_matrix[:closing_slot],
            preferred_element_type=jnp.float32,
        )
        attention_logits = jnp.where(
            allowed[None, None],
            attention_logits * softness_multiplier[opening_slot:closing_slot][None, None, :, None],
            -jnp.inf,
        )
        peak_score = jnp.max(attention_logits, axis=-1, keepdims=True)
        log_total = peak_score + jnp.log(
            jnp.sum(jnp.exp(attention_logits - peak_score), axis=-1, keepdims=True)
        )
        weights_low = jnp.exp(attention_logits - log_total).astype(jnp.bfloat16)
        attended_parts.append(
            jnp.einsum(
                "gjts,sgd->tgjd",
                weights_low,
                value_rows[:closing_slot],
                preferred_element_type=jnp.float32,
            ).astype(jnp.bfloat16)
        )
        total_parts.append(log_total[..., 0])
    attended = jnp.concatenate(attended_parts, axis=0)
    log_totals = jnp.concatenate(total_parts, axis=2)
    flat_out = attended.reshape(tree_len, heads_local * HEAD_SIZE)
    shard_rows = lax.all_gather(cotangent, "ctx", axis=0, tiled=True)
    weight_low = contract_rows(flat_out, shard_rows).astype(jnp.bfloat16)
    asking_heads = jnp.transpose(asking_matrix.reshape(tree_len, heads_local, HEAD_SIZE), (1, 0, 2))
    attended_heads = jnp.transpose(attended.reshape(tree_len, heads_local, HEAD_SIZE), (1, 0, 2))
    (
        weight_low, shard_rows, masks, asking_heads, attended_heads, lookup_matrix, value_rows, log_totals
    ) = lax.optimization_barrier(
        (weight_low, shard_rows, masks, asking_heads, attended_heads, lookup_matrix, value_rows, log_totals)
    )
    weight_total = lax.psum(weight_low, "leaf")
    def backward_part():
        output_gradient = contract_cols(shard_rows, out_weight).astype(jnp.bfloat16)
        grad_heads = jnp.transpose(output_gradient.reshape(tree_len, heads_local, HEAD_SIZE), (1, 0, 2))
        totals_heads = log_totals.reshape(heads_local, tree_len)

        def one_head(head_id, carry):
            key_acc, value_acc, query_grad = carry
            kv_id = head_id // queries_per_group
            keys_all = lax.dynamic_index_in_dim(lookup_matrix, kv_id, axis=1, keepdims=False)
            values_all = lax.dynamic_index_in_dim(value_rows, kv_id, axis=1, keepdims=False)
            query_all = lax.dynamic_index_in_dim(asking_heads, head_id, axis=0, keepdims=False)
            grad_all = lax.dynamic_index_in_dim(grad_heads, head_id, axis=0, keepdims=False)
            own_all = lax.dynamic_index_in_dim(attended_heads, head_id, axis=0, keepdims=False)
            totals_all = lax.dynamic_index_in_dim(totals_heads, head_id, axis=0, keepdims=False)
            key_now = lax.dynamic_index_in_dim(key_acc, kv_id, axis=1, keepdims=False)
            value_now = lax.dynamic_index_in_dim(value_acc, kv_id, axis=1, keepdims=False)
            query_blocks = []
            for block_id in range(block_total):
                opening_slot = block_id * block_len
                closing_slot = opening_slot + block_len
                query_now = query_all[opening_slot:closing_slot]
                keys_now = keys_all[:closing_slot]
                values_now = values_all[:closing_slot]
                line_multiplier = softness_multiplier[opening_slot:closing_slot][:, None]
                attention_logits = jnp.where(
                    masks[block_id], contract_cols(query_now, keys_now) * line_multiplier, -jnp.inf
                )
                attention_probabilities = jnp.exp(
                    attention_logits - totals_all[opening_slot:closing_slot][:, None]
                )
                grad_rows = grad_all[opening_slot:closing_slot]
                own_rows = own_all[opening_slot:closing_slot]
                probability_cotangent = contract_cols(grad_rows, values_now)
                middle_point = jnp.sum(
                    grad_rows.astype(jnp.float32) * own_rows.astype(jnp.float32), axis=1
                )
                logit_cotangent = (
                    attention_probabilities
                    * (probability_cotangent - middle_point[:, None])
                    * line_multiplier
                ).astype(jnp.bfloat16)
                query_blocks.append(
                    jnp.dot(logit_cotangent, keys_now, preferred_element_type=jnp.float32).astype(
                        jnp.bfloat16
                    )
                )
                key_now = key_now.at[:closing_slot].add(contract_rows(logit_cotangent, query_now))
                value_now = value_now.at[:closing_slot].add(
                    contract_rows(attention_probabilities.astype(jnp.bfloat16), grad_rows)
                )
            key_acc = lax.dynamic_update_index_in_dim(key_acc, key_now, kv_id, axis=1)
            value_acc = lax.dynamic_update_index_in_dim(value_acc, value_now, kv_id, axis=1)
            query_grad = lax.dynamic_update_index_in_dim(
                query_grad, jnp.concatenate(query_blocks, axis=0), head_id, axis=0
            )
            return key_acc, value_acc, query_grad

        key_acc, value_acc, query_grad = lax.fori_loop(
            0,
            heads_local,
            one_head,
            (
                jnp.zeros((tree_len, kv_local, HEAD_SIZE), jnp.float32),
                jnp.zeros((tree_len, kv_local, HEAD_SIZE), jnp.float32),
                jnp.zeros((heads_local, tree_len, HEAD_SIZE), jnp.bfloat16),
            ),
        )
        query_grad = jnp.transpose(query_grad, (1, 0, 2)).reshape(
            tree_len, kv_local, queries_per_group, HEAD_SIZE
        )
        gradients = jnp.concatenate(
            [
                query_grad,
                key_acc.astype(jnp.bfloat16)[:, :, None],
                value_acc.astype(jnp.bfloat16)[:, :, None],
            ],
            axis=2,
        )
        gradients = gradients.reshape(tree_len, kv_local * (queries_per_group + 2) * HEAD_SIZE)
        return gradients

    def no_part():
        return jnp.zeros((tree_len, kv_local * (queries_per_group + 2) * HEAD_SIZE), jnp.bfloat16)

    gradients = lax.cond(lax.axis_index("ctx") >= 0, backward_part, no_part)
    returned = lax.all_to_all(gradients, "ctx", split_axis=0, concat_axis=1, tiled=True)
    return (returned, weight_total)


def solution(mesh):
    placed = (
        P(("leaf", "ctx"), None),
        P(("leaf", "ctx"), None),
        P("ctx", None),
        P("leaf", None),
        P("leaf"),
    )
    return jax.shard_map(
        local,
        mesh=mesh,
        in_specs=placed,
        out_specs=(P(("leaf", "ctx"), None), P("ctx", None)),
        check_vma=False,
    )
```
